512 devices in a mesh: tok: 64 (over z, x), head: 8 (over y, core).
Axes of the slice: x: 4, y: 4, z: 16, core: 2. Of those that a mesh axis runs over, the one named last changes fastest.
Arguments:
- tokens: bfloat16 [32768, 2560], P('tok', 'head'), may hold values from -6 to 6
- query_weight: bfloat16 [2560, 2560], P('tok'), may hold values from -0.125 to 0.125
- keyvalue_weight: bfloat16 [2560, 512], P('tok'), may hold values from -0.125 to 0.125
- output_weight: bfloat16 [2560, 2560], P(None, ('head', 'tok')), may hold values from -0.125 to 0.125
- cache: bfloat16 [2048, 2, 128, 256], P(('tok', 'head')), may hold values from -460 to 460
- page_table: int32 [512, 4], P('tok'), may hold values from 0 to 2047, as said below
- parents: int32 [512, 64], P('tok'), may hold values from 0 to 62, as said below
- cache_len: int32 [512], P('tok'), may hold values from 1 to 448, as said below
- accepted_leaf: int32 [512], P('tok'), may hold values from 0 to 63
Outputs:
- attended: bfloat16 [32768, 2560], P('tok', 'head')
- cache_out: bfloat16 [2048, 2, 128, 256], P(('tok', 'head'))
The draws below stay inside these ranges and needn't reach their ends.
Inputs may be any that keep to these rules, and one draw needn't show every extreme that they name: `page_table`: for every d, row d names each of the pages d * 4 to d * 4 + 3 exactly once, so request d's pages all lie on device d (devices counted tok-major, head-minor). parents[r, 0] = 0, and parents[r, i] < i for i >= 1. `cache_len`: roughly half of the requests hold at most 128 cached positions, the others more than 320.
All inputs are finite; a program needn't handle non-finite values.
Results may differ from the reference program's by a relative error of at most 0.014.
The reference program's roundings to bfloat16 on the way count: a program that leaves them out, or rounds other values in their place, can miss the bound.
Values may be sent and summed in bfloat16 or wider, within the bound.
No kernel may reach another device: no remote copies, remote signals or barrier semaphores. Data moves between devices by JAX's collectives and lax.ppermute only.
A program may use at most 64 MiB of HBM per device.

```python
import math
import jax
import jax.numpy as jnp
from jax import lax

D = 2560
HQ = 10
HD = 256
DRAFT = 64
PAGE = 128
NPR = 4
WINDOW = 256
REQ_DEV = 1
P_DEV = 4
CL_MAX = 448
REQUESTS = 512
TOKENS = 32768
PAGES = 2048
N_HEAD = 8


def draw_cache(key, part):
    shape = (PAGES, 2, PAGE, HD)
    return jnp.clip(jax.random.normal(key, shape, jnp.float32), -6.0, 6.0).astype(jnp.bfloat16)


def draw_page_table(key, part):
    device_count = REQUESTS // REQ_DEV
    streams = jax.random.split(key, device_count)

    def shuffle(stream):
        return jax.random.permutation(stream, P_DEV)
    shuffled = jax.vmap(shuffle)(streams)
    offsets = jnp.arange(device_count, dtype=jnp.int32) * P_DEV
    return (shuffled.astype(jnp.int32) + offsets[:, None]).reshape(REQUESTS, NPR)


def draw_parents(key, part):
    node_ids = jnp.arange(DRAFT, dtype=jnp.int32)
    lowest = jnp.maximum(node_ids - 4, 0)
    offset = jax.random.randint(key, (REQUESTS, DRAFT), 0, 4)
    window_span = jnp.maximum(node_ids - lowest, 1)
    parent = lowest[None, :] + offset % window_span[None, :]
    parent = jnp.where(node_ids[None, :] == 0, 0, parent)
    return parent.at[0, DRAFT - 1].set(DRAFT - 2).astype(jnp.int32)


def draw_cache_len(key, part):
    streams = jax.random.split(key, 3)
    is_long = jax.random.permutation(streams[0], REQUESTS) < REQUESTS // 2
    short_len = jax.random.randint(streams[1], (REQUESTS,), 1, PAGE + 1)
    long_len = jax.random.randint(streams[2], (REQUESTS,), CL_MAX - PAGE + 1, CL_MAX + 1)
    lengths = jnp.where(is_long, long_len, short_len)
    return lengths.at[0].set(CL_MAX).at[1].set(1).astype(jnp.int32)


def draw_accepted_leaf(key, part):
    leaves = jax.random.randint(key, (REQUESTS,), 0, DRAFT)
    return leaves.at[0].set(DRAFT - 1).at[1].set(0).astype(jnp.int32)


def levels(own_key, dims, shards, smallest, largest):
    factor_of, own = 1.0, jax.random.fold_in(own_key, 6)
    for axis_at, parts in shards:
        steps = jnp.exp(jax.random.uniform(jax.random.fold_in(own, axis_at), (parts,), jnp.float32, smallest / len(shards), largest / len(shards)))
        factor_of = factor_of * jnp.repeat(steps, dims[axis_at] // parts).reshape([-1 if axis == axis_at else 1 for axis in range(len(dims))])
    return factor_of


def noise(rng, dims, deviation, most, pieces=(), kind=jnp.bfloat16):
    level = levels(rng, dims, pieces, -0.22, 0.18) if pieces else 1.0
    drawn = jax.random.normal(rng, dims, jnp.float32) * deviation * level
    return jnp.minimum(jnp.maximum(drawn, -most), most).astype(kind)


def setup_inputs(seed: int = 0) -> dict:
    keys = jax.random.split(jax.random.key(seed), 10)
    return {
        "tokens": noise(keys[0], (TOKENS, D), 1.0, 6.0, ((0, 64), (1, 8))),
        "query_weight": noise(keys[1], (D, HQ * HD), D ** -0.5, 0.125, ((0, 64),)),
        "keyvalue_weight": noise(keys[2], (D, 2 * HD), D ** -0.5, 0.125, ((0, 64),)),
        "output_weight": noise(keys[3], (HQ * HD, D), (HQ * HD) ** -0.5, 0.125, ((1, 512),)),
        "cache": draw_cache(jax.random.fold_in(keys[9], 71), 0),
        "page_table": draw_page_table(jax.random.fold_in(keys[9], 71), 0),
        "parents": draw_parents(jax.random.fold_in(keys[9], 71), 0),
        "cache_len": draw_cache_len(jax.random.fold_in(keys[9], 71), 0),
        "accepted_leaf": draw_accepted_leaf(jax.random.fold_in(keys[9], 71), 0),
    }


def ancestry(parent_row):
    node_ids = jnp.arange(DRAFT, dtype=jnp.int32)
    link = (parent_row[:, None] == node_ids[None, :]).astype(jnp.float32)
    reach = jnp.minimum(link + jnp.eye(DRAFT, dtype=jnp.float32), 1.0)
    for sweep in range((DRAFT - 1).bit_length()):
        reach = jnp.minimum(jnp.dot(reach, reach, precision=lax.Precision.HIGHEST), 1.0)
    depth = (lax.optimization_barrier(jnp.sum(reach, axis=1)) - 1.0).astype(jnp.int32)
    return (reach, depth)

def rotate(values, position):
    half = HD // 4
    freq = jnp.exp(jnp.arange(half, dtype=jnp.float32) * (-2.0 * math.log(10000.0) / (HD // 2)))
    angle = position.astype(jnp.float32)[..., None] * freq
    cosine = jnp.cos(angle)
    sine = jnp.sin(angle)
    first = values[..., :half]
    second = values[..., half:2 * half]
    return jnp.concatenate([first * cosine - second * sine, second * cosine + first * sine, values[..., 2 * half:]], axis=-1)

def attend(queries, cache_keys, cache_values, tree_keys, tree_values, lengths, position, reach):
    window_span = cache_keys.shape[1]
    slot_ids = jnp.arange(window_span, dtype=jnp.int32)
    visible = (slot_ids[None, None, :] < lengths[:, None, None]) & (slot_ids[None, None, :] > position[:, :, None] - WINDOW)
    cache_scores = jnp.einsum('rnhd,rcd->rhnc', queries.astype(jnp.float32), cache_keys.astype(jnp.float32))
    tree_scores = jnp.einsum('rnhd,rmd->rhnm', queries.astype(jnp.float32), tree_keys.astype(jnp.float32))
    cache_scores = jnp.where(visible[:, None], cache_scores, -1e+30)
    tree_scores = jnp.where(reach[:, None] > 0.5, tree_scores, -1e+30)
    row_peak = jnp.maximum(lax.optimization_barrier(jnp.max(cache_scores, axis=-1)), lax.optimization_barrier(jnp.max(tree_scores, axis=-1)))[..., None]
    cache_weights = jnp.exp(cache_scores - row_peak)
    tree_weights = jnp.exp(tree_scores - row_peak)
    denominator = lax.optimization_barrier(jnp.sum(cache_weights, axis=-1, keepdims=True)) + lax.optimization_barrier(jnp.sum(tree_weights, axis=-1, keepdims=True))
    cache_weights = (cache_weights / denominator).astype(jnp.bfloat16)
    tree_weights = (tree_weights / denominator).astype(jnp.bfloat16)
    result = jnp.einsum('rhnc,rcd->rnhd', cache_weights.astype(jnp.float32), cache_values.astype(jnp.float32))
    result = result + jnp.einsum('rhnm,rmd->rnhd', tree_weights.astype(jnp.float32), tree_values.astype(jnp.float32))
    return result.astype(jnp.bfloat16)

def refresh(logical_pages, length, leaf, reach, depth, new_keys, new_values):
    count = logical_pages.shape[0] * logical_pages.shape[2]
    logical = jnp.transpose(logical_pages, (1, 0, 2, 3)).reshape(2, count, HD)
    slot_ids = jnp.arange(count, dtype=jnp.int32)
    on_path = reach[leaf]
    selector = ((on_path[None, :] > 0.5) & (depth[None, :] == slot_ids[:, None] - length)).astype(jnp.float32)
    placed_keys = jnp.dot(selector, new_keys.astype(jnp.float32), precision=lax.Precision.HIGHEST)
    placed_values = jnp.dot(selector, new_values.astype(jnp.float32), precision=lax.Precision.HIGHEST)
    placed = jnp.stack([placed_keys, placed_values]).astype(jnp.bfloat16)
    written = lax.optimization_barrier(jnp.sum(selector, axis=1)) > 0.5
    logical = jnp.where(written[None, :, None], placed, logical)
    return jnp.transpose(logical.reshape(2, logical_pages.shape[0], logical_pages.shape[2], HD), (1, 0, 2, 3))

def reference(tokens, query_weight, keyvalue_weight, output_weight, cache, page_table, parents, cache_len, accepted_leaf):
    wide = tokens.astype(jnp.float32)
    mean_square = lax.optimization_barrier(jnp.mean(wide * wide, axis=1, keepdims=True))
    normed = (wide * lax.rsqrt(mean_square + 1e-06)).astype(jnp.bfloat16)
    reach, depth = jax.vmap(ancestry)(parents)
    position = cache_len[:, None] + depth
    flat_pos = position.reshape(TOKENS)
    queries = jnp.dot(normed, query_weight, preferred_element_type=jnp.float32).reshape(TOKENS, HQ, HD)
    queries = (rotate(queries, flat_pos[:, None]) * HD ** (-0.5)).astype(jnp.bfloat16)
    queries = queries.reshape(REQUESTS, DRAFT, HQ, HD)
    projected = jnp.dot(normed, keyvalue_weight, preferred_element_type=jnp.float32)
    tree_keys = rotate(projected[:, :HD], flat_pos).astype(jnp.bfloat16).reshape(REQUESTS, DRAFT, HD)
    tree_values = projected[:, HD:].astype(jnp.bfloat16).reshape(REQUESTS, DRAFT, HD)

    def one_request(packed):
        query_block, key_block, value_block, table_row, length, pos_row, reach_block = packed
        page_blocks = jnp.take(cache, table_row, axis=0)
        cache_keys = page_blocks[:, 0].reshape(NPR * PAGE, HD)
        cache_values = page_blocks[:, 1].reshape(NPR * PAGE, HD)
        return attend(query_block[None], cache_keys[None], cache_values[None], key_block[None], value_block[None], length[None], pos_row[None], reach_block[None])[0]
    mixed = lax.map(one_request, (queries, tree_keys, tree_values, page_table, cache_len, position, reach))
    mixed = mixed.reshape(TOKENS, HQ, HD)
    per_group = (HQ + N_HEAD - 1) // N_HEAD
    head_rows = output_weight.reshape(HQ, HD, D)
    summed = jnp.zeros((TOKENS, D), jnp.float32)
    for group in range(N_HEAD):
        head_ids = [group + N_HEAD * slot for slot in range(per_group) if group + N_HEAD * slot < HQ]
        if head_ids:
            chosen = jnp.array(head_ids, dtype=jnp.int32)
            columns = jnp.take(mixed, chosen, axis=1).reshape(TOKENS, len(head_ids) * HD)
            weights = jnp.take(head_rows, chosen, axis=0).reshape(len(head_ids) * HD, D)
            partial_value = jnp.dot(columns, weights, preferred_element_type=jnp.float32).astype(jnp.bfloat16)
            summed = summed + partial_value.astype(jnp.float32)
    attended = summed.astype(jnp.bfloat16)

    def one_update(packed):
        table_row, length, leaf, reach_block, depth_row, key_block, value_block = packed
        page_blocks = jnp.take(cache, table_row, axis=0)
        return refresh(page_blocks, length, leaf, reach_block, depth_row, key_block, value_block)
    new_pages = lax.map(one_update, (page_table, cache_len, accepted_leaf, reach, depth, tree_keys, tree_values))
    cache_out = cache.at[page_table.reshape(-1)].set(new_pages.reshape(REQUESTS * NPR, 2, PAGE, HD))
    return (attended, cache_out)
```

```python
import math

import jax
import jax.numpy as jnp
from jax import lax
from jax.sharding import PartitionSpec as P

HQ = 10
HD = 256
DRAFT = 64
PAGE = 128
NPR = 4
WINDOW = 256


def ancestry(parent_row):
    node_ids = jnp.arange(DRAFT, dtype=jnp.int32)
    link = (parent_row[:, None] == node_ids[None, :]).astype(jnp.float32)
    reach = jnp.minimum(link + jnp.eye(DRAFT, dtype=jnp.float32), 1.0)
    for sweep in range((DRAFT - 1).bit_length()):
        reach = jnp.minimum(jnp.dot(reach, reach, precision=lax.Precision.HIGHEST), 1.0)
    depth = (jnp.sum(reach, axis=1) - 1.0).astype(jnp.int32)
    return (reach, depth)


def rotate(values, position):
    half = HD // 4
    freq = jnp.exp(jnp.arange(half, dtype=jnp.float32) * (-2.0 * math.log(10000.0) / (HD // 2)))
    angle = position.astype(jnp.float32)[..., None] * freq
    cosine = jnp.cos(angle)
    sine = jnp.sin(angle)
    first = values[..., :half]
    second = values[..., half : 2 * half]
    return jnp.concatenate(
        [first * cosine - second * sine, second * cosine + first * sine, values[..., 2 * half :]],
        axis=-1,
    )


def attend(queries, cache_keys, cache_values, tree_keys, tree_values, lengths, position, reach):
    window_span = cache_keys.shape[1]
    slot_ids = jnp.arange(window_span, dtype=jnp.int32)
    visible = (slot_ids[None, None, :] < lengths[:, None, None]) & (
        slot_ids[None, None, :] > position[:, :, None] - WINDOW
    )
    cache_scores = jnp.einsum(
        "rnhd,rcd->rhnc", queries, cache_keys, preferred_element_type=jnp.float32
    )
    tree_scores = jnp.einsum(
        "rnhd,rmd->rhnm", queries, tree_keys, preferred_element_type=jnp.float32
    )
    cache_scores = jnp.where(visible[:, None], cache_scores, -1e30)
    tree_scores = jnp.where(reach[:, None] > 0.5, tree_scores, -1e30)
    row_peak = jnp.maximum(jnp.max(cache_scores, axis=-1), jnp.max(tree_scores, axis=-1))[..., None]
    cache_weights = jnp.exp(cache_scores - row_peak)
    tree_weights = jnp.exp(tree_scores - row_peak)
    denominator = jnp.sum(cache_weights, axis=-1, keepdims=True) + jnp.sum(
        tree_weights, axis=-1, keepdims=True
    )
    cache_weights = (cache_weights / denominator).astype(jnp.bfloat16)
    tree_weights = (tree_weights / denominator).astype(jnp.bfloat16)
    result = jnp.einsum(
        "rhnc,rcd->rnhd", cache_weights, cache_values, preferred_element_type=jnp.float32
    )
    result = result + jnp.einsum(
        "rhnm,rmd->rnhd", tree_weights, tree_values, preferred_element_type=jnp.float32
    )
    return result.astype(jnp.bfloat16)


def refresh(logical_pages, length, leaf, reach, depth, new_keys, new_values):
    count = logical_pages.shape[0] * logical_pages.shape[2]
    logical = jnp.transpose(logical_pages, (1, 0, 2, 3)).reshape(2, count, HD)
    slot_ids = jnp.arange(count, dtype=jnp.int32)
    on_path = reach[leaf]
    selector = ((on_path[None, :] > 0.5) & (depth[None, :] == slot_ids[:, None] - length)).astype(
        jnp.float32
    )
    placed_keys = jnp.dot(selector, new_keys.astype(jnp.float32), precision=lax.Precision.HIGHEST)
    placed_values = jnp.dot(
        selector, new_values.astype(jnp.float32), precision=lax.Precision.HIGHEST
    )
    placed = jnp.stack([placed_keys, placed_values]).astype(jnp.bfloat16)
    written = jnp.sum(selector, axis=1) > 0.5
    logical = jnp.where(written[None, :, None], placed, logical)
    return jnp.transpose(
        logical.reshape(2, logical_pages.shape[0], logical_pages.shape[2], HD), (1, 0, 2, 3)
    )


def shards(
    tokens,
    query_weight,
    keyvalue_weight,
    output_weight,
    cache,
    page_table,
    parents,
    cache_len,
    accepted_leaf,
):
    head_count = lax.axis_size("head")
    head_index = lax.axis_index("head")
    tok_index = lax.axis_index("tok")
    requests = parents.shape[0]
    assert requests == head_count
    pages_dev = cache.shape[0]
    part_rows = query_weight.shape[0]
    q_cols = (HQ * HD) // head_count
    kv_cols = (2 * HD) // head_count
    out_cols = output_weight.shape[1]
    wq_piece = lax.dynamic_slice_in_dim(query_weight, head_index * q_cols, q_cols, axis=1)
    wkv_piece = lax.dynamic_slice_in_dim(keyvalue_weight, head_index * kv_cols, kv_cols, axis=1)
    flat = jnp.concatenate(
        [wq_piece.reshape(-1), wkv_piece.reshape(-1), output_weight.reshape(-1)]
    )
    stacked = lax.all_gather(flat, "tok", axis=0, tiled=False)
    tok_count = stacked.shape[0]
    n_q = part_rows * q_cols
    n_kv = part_rows * kv_cols
    wq_cols = stacked[:, :n_q].reshape(tok_count * part_rows, q_cols)
    wkv_cols = stacked[:, n_q : n_q + n_kv].reshape(tok_count * part_rows, kv_cols)
    wo_cols = (
        stacked[:, n_q + n_kv :]
        .reshape(tok_count, HQ * HD, out_cols)
        .transpose(1, 0, 2)
        .reshape(HQ * HD, tok_count * out_cols)
    )
    gathered = lax.all_gather(tokens, "head", axis=1, tiled=True)
    wide = gathered.astype(jnp.float32)
    mean_square = jnp.mean(wide * wide, axis=1, keepdims=True)
    normed = (wide * lax.rsqrt(mean_square + 1e-06)).astype(jnp.bfloat16)
    q_part = jnp.dot(normed, wq_cols, preferred_element_type=jnp.float32)
    kv_part = jnp.dot(normed, wkv_cols, preferred_element_type=jnp.float32)
    both = jnp.concatenate([q_part, kv_part], axis=1)
    mine = lax.all_to_all(both, "head", 0, 1, tiled=True)
    mine = mine.reshape(DRAFT, head_count, q_cols + kv_cols)
    q_pre = mine[:, :, :q_cols].reshape(DRAFT, HQ, HD)
    kv_pre = mine[:, :, q_cols:].reshape(DRAFT, 2 * HD)
    parent_row = lax.dynamic_index_in_dim(parents, head_index, 0, keepdims=False)
    length = lax.dynamic_index_in_dim(cache_len, head_index, 0, keepdims=False)
    leaf = lax.dynamic_index_in_dim(accepted_leaf, head_index, 0, keepdims=False)
    reach, depth = ancestry(parent_row)
    position = length + depth
    queries = (rotate(q_pre, position[:, None]) * HD ** (-0.5)).astype(jnp.bfloat16)
    tree_keys = rotate(kv_pre[:, :HD], position).astype(jnp.bfloat16)
    tree_values = kv_pre[:, HD:].astype(jnp.bfloat16)
    device = tok_index * head_count + head_index
    own_table = (
        lax.dynamic_index_in_dim(page_table, head_index, 0, keepdims=False) - device * pages_dev
    )
    own_pages = jnp.take(cache, own_table, axis=0)
    cache_keys = own_pages[:, 0].reshape(NPR * PAGE, HD)
    cache_values = own_pages[:, 1].reshape(NPR * PAGE, HD)
    result = attend(
        queries[None],
        cache_keys[None],
        cache_values[None],
        tree_keys[None],
        tree_values[None],
        length[None],
        position[None],
        reach[None],
    )
    mixed = lax.all_gather(result.reshape(DRAFT, HQ * HD), "head", axis=0, tiled=True)
    summed = jnp.zeros((mixed.shape[0], wo_cols.shape[1]), jnp.float32)
    for group in range(head_count):
        head_ids = [k for k in range(group, HQ, head_count)]
        if not head_ids:
            continue
        columns = jnp.concatenate([mixed[:, k * HD : (k + 1) * HD] for k in head_ids], axis=1)
        rows = jnp.concatenate([wo_cols[k * HD : (k + 1) * HD] for k in head_ids], axis=0)
        partial_value = jnp.dot(columns, rows, preferred_element_type=jnp.float32)
        summed = summed + partial_value.astype(jnp.bfloat16).astype(jnp.float32)
    attended = summed.astype(jnp.bfloat16)
    new_pages = refresh(own_pages, length, leaf, reach, depth, tree_keys, tree_values)
    matches = (own_table[:, None] == jnp.arange(pages_dev, dtype=jnp.int32)[None, :]).astype(
        jnp.int32
    )
    inverse = jnp.sum(matches * jnp.arange(pages_dev, dtype=jnp.int32)[:, None], axis=0)
    cache_out = jnp.take(new_pages, inverse, axis=0)
    return (attended, cache_out)


def solution(mesh):
    in_specs = (
        P("tok", "head"),
        P("tok", None),
        P("tok", None),
        P(None, ("head", "tok")),
        P(("tok", "head"), None, None, None),
        P("tok", None),
        P("tok", None),
        P("tok"),
        P("tok"),
    )
    out_specs = (P("tok", "head"), P(("tok", "head"), None, None, None))
    return jax.shard_map(shards, mesh=mesh, in_specs=in_specs, out_specs=out_specs, check_vma=False)
```

```python
import math

import jax
import jax.numpy as jnp
from jax import lax
from jax.sharding import Mesh, PartitionSpec as P

HQ = 10
HD = 256
DRAFT = 64
PAGE = 128
NPR = 4
WINDOW = 256


def ancestry(parent_row):
    node_ids = jnp.arange(DRAFT, dtype=jnp.int32)
    link = (parent_row[:, None] == node_ids[None, :]).astype(jnp.float32)
    reach = jnp.minimum(link + jnp.eye(DRAFT, dtype=jnp.float32), 1.0)
    for sweep in range((DRAFT - 1).bit_length()):
        reach = jnp.minimum(jnp.dot(reach, reach, precision=lax.Precision.HIGHEST), 1.0)
    depth = (jnp.sum(reach, axis=1) - 1.0).astype(jnp.int32)
    return (reach, depth)


def rotate(values, position):
    half = HD // 4
    freq = jnp.exp(jnp.arange(half, dtype=jnp.float32) * (-2.0 * math.log(10000.0) / (HD // 2)))
    angle = position.astype(jnp.float32)[..., None] * freq
    cosine = jnp.cos(angle)
    sine = jnp.sin(angle)
    first = values[..., :half]
    second = values[..., half : 2 * half]
    return jnp.concatenate(
        [first * cosine - second * sine, second * cosine + first * sine, values[..., 2 * half :]],
        axis=-1,
    )


def attend(queries, cache_keys, cache_values, tree_keys, tree_values, lengths, position, reach):
    window_span = cache_keys.shape[1]
    slot_ids = jnp.arange(window_span, dtype=jnp.int32)
    visible = (slot_ids[None, None, :] < lengths[:, None, None]) & (
        slot_ids[None, None, :] > position[:, :, None] - WINDOW
    )
    cache_scores = jnp.einsum(
        "rnhd,rcd->rhnc", queries, cache_keys, preferred_element_type=jnp.float32
    )
    tree_scores = jnp.einsum(
        "rnhd,rmd->rhnm", queries, tree_keys, preferred_element_type=jnp.float32
    )
    cache_scores = jnp.where(visible[:, None], cache_scores, -1e30)
    tree_scores = jnp.where(reach[:, None] > 0.5, tree_scores, -1e30)
    row_peak = jnp.maximum(jnp.max(cache_scores, axis=-1), jnp.max(tree_scores, axis=-1))[..., None]
    cache_weights = jnp.exp(cache_scores - row_peak)
    tree_weights = jnp.exp(tree_scores - row_peak)
    denominator = jnp.sum(cache_weights, axis=-1, keepdims=True) + jnp.sum(
        tree_weights, axis=-1, keepdims=True
    )
    cache_weights = (cache_weights / denominator).astype(jnp.bfloat16)
    tree_weights = (tree_weights / denominator).astype(jnp.bfloat16)
    result = jnp.einsum(
        "rhnc,rcd->rnhd", cache_weights, cache_values, preferred_element_type=jnp.float32
    )
    result = result + jnp.einsum(
        "rhnm,rmd->rnhd", tree_weights, tree_values, preferred_element_type=jnp.float32
    )
    return result.astype(jnp.bfloat16)


def refresh(logical_pages, length, leaf, reach, depth, new_keys, new_values):
    count = logical_pages.shape[0] * logical_pages.shape[2]
    logical = jnp.transpose(logical_pages, (1, 0, 2, 3)).reshape(2, count, HD)
    slot_ids = jnp.arange(count, dtype=jnp.int32)
    on_path = reach[leaf]
    selector = ((on_path[None, :] > 0.5) & (depth[None, :] == slot_ids[:, None] - length)).astype(
        jnp.float32
    )
    placed_keys = jnp.dot(selector, new_keys.astype(jnp.float32), precision=lax.Precision.HIGHEST)
    placed_values = jnp.dot(
        selector, new_values.astype(jnp.float32), precision=lax.Precision.HIGHEST
    )
    placed = jnp.stack([placed_keys, placed_values]).astype(jnp.bfloat16)
    written = jnp.sum(selector, axis=1) > 0.5
    logical = jnp.where(written[None, :, None], placed, logical)
    return jnp.transpose(
        logical.reshape(2, logical_pages.shape[0], logical_pages.shape[2], HD), (1, 0, 2, 3)
    )


def ring_gather(piece, axis):
    size = lax.axis_size(axis)
    if size == 1:
        return piece[None]
    index = lax.axis_index(axis)
    by_offset = {0: piece}
    ahead = piece
    behind = piece
    for step in range(1, size // 2 + 1):
        ahead = lax.ppermute(ahead, axis, [(i, (i + 1) % size) for i in range(size)])
        by_offset[size - step] = ahead
        if step <= (size - 1) // 2:
            behind = lax.ppermute(behind, axis, [(i, (i - 1) % size) for i in range(size)])
            by_offset[step] = behind
    ordered = jnp.stack([by_offset[k] for k in range(size)])
    doubled = jnp.concatenate([ordered, ordered], axis=0)
    return lax.dynamic_slice_in_dim(doubled, size - index, size, axis=0)


def grid_gather(piece):
    inner = ring_gather(piece, "tx")
    outer = ring_gather(inner.reshape(-1), "tz")
    return outer.reshape(-1, piece.shape[0])


def shards(
    tokens,
    query_weight,
    keyvalue_weight,
    output_weight,
    cache,
    page_table,
    parents,
    cache_len,
    accepted_leaf,
):
    head_count = lax.axis_size("head")
    head_index = lax.axis_index("head")
    tok_index = lax.axis_index("tz") * lax.axis_size("tx") + lax.axis_index("tx")
    requests = parents.shape[0]
    assert requests == head_count
    pages_dev = cache.shape[0]
    part_rows = query_weight.shape[0]
    q_cols = (HQ * HD) // head_count
    kv_cols = (2 * HD) // head_count
    out_cols = output_weight.shape[1]
    wq_piece = lax.dynamic_slice_in_dim(query_weight, head_index * q_cols, q_cols, axis=1)
    wkv_piece = lax.dynamic_slice_in_dim(keyvalue_weight, head_index * kv_cols, kv_cols, axis=1)
    flat = jnp.concatenate(
        [wq_piece.reshape(-1), wkv_piece.reshape(-1), output_weight.reshape(-1)]
    )
    stacked = grid_gather(flat)
    tok_count = stacked.shape[0]
    n_q = part_rows * q_cols
    n_kv = part_rows * kv_cols
    wq_cols = stacked[:, :n_q].reshape(tok_count * part_rows, q_cols)
    wkv_cols = stacked[:, n_q : n_q + n_kv].reshape(tok_count * part_rows, kv_cols)
    wo_cols = (
        stacked[:, n_q + n_kv :]
        .reshape(tok_count, HQ * HD, out_cols)
        .transpose(1, 0, 2)
        .reshape(HQ * HD, tok_count * out_cols)
    )
    gathered = lax.all_gather(tokens, "head", axis=1, tiled=True)
    wide = gathered.astype(jnp.float32)
    mean_square = jnp.mean(wide * wide, axis=1, keepdims=True)
    normed = (wide * lax.rsqrt(mean_square + 1e-06)).astype(jnp.bfloat16)
    q_part = jnp.dot(normed, wq_cols, preferred_element_type=jnp.float32)
    kv_part = jnp.dot(normed, wkv_cols, preferred_element_type=jnp.float32)
    both = jnp.concatenate([q_part, kv_part], axis=1)
    mine = lax.all_to_all(both, "head", 0, 1, tiled=True)
    mine = mine.reshape(DRAFT, head_count, q_cols + kv_cols)
    q_pre = mine[:, :, :q_cols].reshape(DRAFT, HQ, HD)
    kv_pre = mine[:, :, q_cols:].reshape(DRAFT, 2 * HD)
    parent_row = lax.dynamic_index_in_dim(parents, head_index, 0, keepdims=False)
    length = lax.dynamic_index_in_dim(cache_len, head_index, 0, keepdims=False)
    leaf = lax.dynamic_index_in_dim(accepted_leaf, head_index, 0, keepdims=False)
    reach, depth = ancestry(parent_row)
    position = length + depth
    queries = (rotate(q_pre, position[:, None]) * HD ** (-0.5)).astype(jnp.bfloat16)
    tree_keys = rotate(kv_pre[:, :HD], position).astype(jnp.bfloat16)
    tree_values = kv_pre[:, HD:].astype(jnp.bfloat16)
    device = tok_index * head_count + head_index
    own_table = (
        lax.dynamic_index_in_dim(page_table, head_index, 0, keepdims=False) - device * pages_dev
    )
    own_pages = jnp.take(cache, own_table, axis=0)
    cache_keys = own_pages[:, 0].reshape(NPR * PAGE, HD)
    cache_values = own_pages[:, 1].reshape(NPR * PAGE, HD)
    result = attend(
        queries[None],
        cache_keys[None],
        cache_values[None],
        tree_keys[None],
        tree_values[None],
        length[None],
        position[None],
        reach[None],
    )
    mixed = lax.all_gather(result.reshape(DRAFT, HQ * HD), "head", axis=0, tiled=True)
    summed = jnp.zeros((mixed.shape[0], wo_cols.shape[1]), jnp.float32)
    for group in range(head_count):
        head_ids = [k for k in range(group, HQ, head_count)]
        if not head_ids:
            continue
        columns = jnp.concatenate([mixed[:, k * HD : (k + 1) * HD] for k in head_ids], axis=1)
        rows = jnp.concatenate([wo_cols[k * HD : (k + 1) * HD] for k in head_ids], axis=0)
        partial_value = jnp.dot(columns, rows, preferred_element_type=jnp.float32)
        summed = summed + partial_value.astype(jnp.bfloat16).astype(jnp.float32)
    attended = summed.astype(jnp.bfloat16)
    new_pages = refresh(own_pages, length, leaf, reach, depth, tree_keys, tree_values)
    matches = (own_table[:, None] == jnp.arange(pages_dev, dtype=jnp.int32)[None, :]).astype(
        jnp.int32
    )
    inverse = jnp.sum(matches * jnp.arange(pages_dev, dtype=jnp.int32)[:, None], axis=0)
    cache_out = jnp.take(new_pages, inverse, axis=0)
    return (attended, cache_out)


def solution(mesh):
    tok_size = mesh.shape["tok"]
    tx_size = 4 if tok_size % 4 == 0 else tok_size
    grid = Mesh(
        mesh.devices.reshape(tok_size // tx_size, tx_size, mesh.shape["head"]),
        ("tz", "tx", "head"),
    )
    tok = ("tz", "tx")
    in_specs = (
        P(tok, "head"),
        P(tok, None),
        P(tok, None),
        P(None, ("head",) + tok),
        P(tok + ("head",), None, None, None),
        P(tok, None),
        P(tok, None),
        P(tok),
        P(tok),
    )
    out_specs = (P(tok, "head"), P(tok + ("head",), None, None, None))
    return jax.shard_map(shards, mesh=grid, in_specs=in_specs, out_specs=out_specs, check_vma=False)
```

```python
import math

import jax
import jax.numpy as jnp
from jax import lax
from jax.sharding import PartitionSpec as P

HQ = 10
HD = 256
DRAFT = 64
PAGE = 128
NPR = 4
WINDOW = 256


def ancestry(parent_row):
    node_ids = jnp.arange(DRAFT, dtype=jnp.int32)
    link = (parent_row[:, None] == node_ids[None, :]).astype(jnp.float32)
    reach = jnp.minimum(link + jnp.eye(DRAFT, dtype=jnp.float32), 1.0)
    for sweep in range((DRAFT - 1).bit_length()):
        reach = jnp.minimum(jnp.dot(reach, reach, precision=lax.Precision.HIGHEST), 1.0)
    depth = (jnp.sum(reach, axis=1) - 1.0).astype(jnp.int32)
    return (reach, depth)


def rotate(values, position):
    half = HD // 4
    freq = jnp.exp(jnp.arange(half, dtype=jnp.float32) * (-2.0 * math.log(10000.0) / (HD // 2)))
    angle = position.astype(jnp.float32)[..., None] * freq
    cosine = jnp.cos(angle)
    sine = jnp.sin(angle)
    first = values[..., :half]
    second = values[..., half : 2 * half]
    return jnp.concatenate(
        [first * cosine - second * sine, second * cosine + first * sine, values[..., 2 * half :]],
        axis=-1,
    )


def attend(queries, cache_keys, cache_values, tree_keys, tree_values, lengths, position, reach):
    window_span = cache_keys.shape[1]
    slot_ids = jnp.arange(window_span, dtype=jnp.int32)
    visible = (slot_ids[None, None, :] < lengths[:, None, None]) & (
        slot_ids[None, None, :] > position[:, :, None] - WINDOW
    )
    cache_scores = jnp.einsum(
        "rnhd,rcd->rhnc", queries, cache_keys, preferred_element_type=jnp.float32
    )
    tree_scores = jnp.einsum(
        "rnhd,rmd->rhnm", queries, tree_keys, preferred_element_type=jnp.float32
    )
    cache_scores = jnp.where(visible[:, None], cache_scores, -1e30)
    tree_scores = jnp.where(reach[:, None] > 0.5, tree_scores, -1e30)
    row_peak = jnp.maximum(jnp.max(cache_scores, axis=-1), jnp.max(tree_scores, axis=-1))[..., None]
    cache_weights = jnp.exp(cache_scores - row_peak)
    tree_weights = jnp.exp(tree_scores - row_peak)
    denominator = jnp.sum(cache_weights, axis=-1, keepdims=True) + jnp.sum(
        tree_weights, axis=-1, keepdims=True
    )
    cache_weights = (cache_weights / denominator).astype(jnp.bfloat16)
    tree_weights = (tree_weights / denominator).astype(jnp.bfloat16)
    result = jnp.einsum(
        "rhnc,rcd->rnhd", cache_weights, cache_values, preferred_element_type=jnp.float32
    )
    result = result + jnp.einsum(
        "rhnm,rmd->rnhd", tree_weights, tree_values, preferred_element_type=jnp.float32
    )
    return result.astype(jnp.bfloat16)


def refresh(logical_pages, length, leaf, reach, depth, new_keys, new_values):
    count = logical_pages.shape[0] * logical_pages.shape[2]
    logical = jnp.transpose(logical_pages, (1, 0, 2, 3)).reshape(2, count, HD)
    slot_ids = jnp.arange(count, dtype=jnp.int32)
    on_path = reach[leaf]
    selector = ((on_path[None, :] > 0.5) & (depth[None, :] == slot_ids[:, None] - length)).astype(
        jnp.float32
    )
    placed_keys = jnp.dot(selector, new_keys.astype(jnp.float32), precision=lax.Precision.HIGHEST)
    placed_values = jnp.dot(
        selector, new_values.astype(jnp.float32), precision=lax.Precision.HIGHEST
    )
    placed = jnp.stack([placed_keys, placed_values]).astype(jnp.bfloat16)
    written = jnp.sum(selector, axis=1) > 0.5
    logical = jnp.where(written[None, :, None], placed, logical)
    return jnp.transpose(
        logical.reshape(2, logical_pages.shape[0], logical_pages.shape[2], HD), (1, 0, 2, 3)
    )


def shards(
    tokens,
    query_weight,
    keyvalue_weight,
    output_weight,
    cache,
    page_table,
    parents,
    cache_len,
    accepted_leaf,
):
    head_count = lax.axis_size("head")
    head_index = lax.axis_index("head")
    tok_index = lax.axis_index("tok")
    requests = parents.shape[0]
    assert requests == head_count
    pages_dev = cache.shape[0]
    part_rows = query_weight.shape[0]
    q_cols = (HQ * HD) // head_count
    kv_cols = (2 * HD) // head_count
    out_cols = output_weight.shape[1]
    wq_piece = lax.dynamic_slice_in_dim(query_weight, head_index * q_cols, q_cols, axis=1)
    wkv_piece = lax.dynamic_slice_in_dim(keyvalue_weight, head_index * kv_cols, kv_cols, axis=1)
    flat = jnp.concatenate(
        [wq_piece.reshape(-1), wkv_piece.reshape(-1), output_weight.reshape(-1)]
    )
    tok_count = lax.axis_size("tok")
    lanes = 128
    tiles = flat.reshape(-1, lanes)
    copies = jnp.broadcast_to(tiles[None], (tok_count,) + tiles.shape)
    stacked = lax.all_to_all(copies, "tok", 0, 0, tiled=True).reshape(tok_count, -1)
    n_q = part_rows * q_cols
    n_kv = part_rows * kv_cols
    wq_cols = stacked[:, :n_q].reshape(tok_count * part_rows, q_cols)
    wkv_cols = stacked[:, n_q : n_q + n_kv].reshape(tok_count * part_rows, kv_cols)
    wo_cols = (
        stacked[:, n_q + n_kv :]
        .reshape(tok_count, HQ * HD, out_cols)
        .transpose(1, 0, 2)
        .reshape(HQ * HD, tok_count * out_cols)
    )
    gathered = lax.all_gather(tokens, "head", axis=1, tiled=True)
    wide = gathered.astype(jnp.float32)
    mean_square = jnp.mean(wide * wide, axis=1, keepdims=True)
    normed = (wide * lax.rsqrt(mean_square + 1e-06)).astype(jnp.bfloat16)
    q_part = jnp.dot(normed, wq_cols, preferred_element_type=jnp.float32)
    kv_part = jnp.dot(normed, wkv_cols, preferred_element_type=jnp.float32)
    both = jnp.concatenate([q_part, kv_part], axis=1)
    mine = lax.all_to_all(both, "head", 0, 1, tiled=True)
    mine = mine.reshape(DRAFT, head_count, q_cols + kv_cols)
    q_pre = mine[:, :, :q_cols].reshape(DRAFT, HQ, HD)
    kv_pre = mine[:, :, q_cols:].reshape(DRAFT, 2 * HD)
    parent_row = lax.dynamic_index_in_dim(parents, head_index, 0, keepdims=False)
    length = lax.dynamic_index_in_dim(cache_len, head_index, 0, keepdims=False)
    leaf = lax.dynamic_index_in_dim(accepted_leaf, head_index, 0, keepdims=False)
    reach, depth = ancestry(parent_row)
    position = length + depth
    queries = (rotate(q_pre, position[:, None]) * HD ** (-0.5)).astype(jnp.bfloat16)
    tree_keys = rotate(kv_pre[:, :HD], position).astype(jnp.bfloat16)
    tree_values = kv_pre[:, HD:].astype(jnp.bfloat16)
    device = tok_index * head_count + head_index
    own_table = (
        lax.dynamic_index_in_dim(page_table, head_index, 0, keepdims=False) - device * pages_dev
    )
    own_pages = jnp.take(cache, own_table, axis=0)
    cache_keys = own_pages[:, 0].reshape(NPR * PAGE, HD)
    cache_values = own_pages[:, 1].reshape(NPR * PAGE, HD)
    result = attend(
        queries[None],
        cache_keys[None],
        cache_values[None],
        tree_keys[None],
        tree_values[None],
        length[None],
        position[None],
        reach[None],
    )
    mixed = lax.all_gather(result.reshape(DRAFT, HQ * HD), "head", axis=0, tiled=True)
    summed = jnp.zeros((mixed.shape[0], wo_cols.shape[1]), jnp.float32)
    for group in range(head_count):
        head_ids = [k for k in range(group, HQ, head_count)]
        if not head_ids:
            continue
        columns = jnp.concatenate([mixed[:, k * HD : (k + 1) * HD] for k in head_ids], axis=1)
        rows = jnp.concatenate([wo_cols[k * HD : (k + 1) * HD] for k in head_ids], axis=0)
        partial_value = jnp.dot(columns, rows, preferred_element_type=jnp.float32)
        summed = summed + partial_value.astype(jnp.bfloat16).astype(jnp.float32)
    attended = summed.astype(jnp.bfloat16)
    new_pages = refresh(own_pages, length, leaf, reach, depth, tree_keys, tree_values)
    matches = (own_table[:, None] == jnp.arange(pages_dev, dtype=jnp.int32)[None, :]).astype(
        jnp.int32
    )
    inverse = jnp.sum(matches * jnp.arange(pages_dev, dtype=jnp.int32)[:, None], axis=0)
    cache_out = jnp.take(new_pages, inverse, axis=0)
    return (attended, cache_out)


def solution(mesh):
    in_specs = (
        P("tok", "head"),
        P("tok", None),
        P("tok", None),
        P(None, ("head", "tok")),
        P(("tok", "head"), None, None, None),
        P("tok", None),
        P("tok", None),
        P("tok"),
        P("tok"),
    )
    out_specs = (P("tok", "head"), P(("tok", "head"), None, None, None))
    return jax.shard_map(shards, mesh=mesh, in_specs=in_specs, out_specs=out_specs, check_vma=False)
```

```python
import math

import jax
import jax.numpy as jnp
from jax import lax
from jax.sharding import Mesh, PartitionSpec as P

HQ = 10
HD = 256
DRAFT = 64
PAGE = 128
NPR = 4
WINDOW = 256


def ancestry(parent_row):
    node_ids = jnp.arange(DRAFT, dtype=jnp.int32)
    link = (parent_row[:, None] == node_ids[None, :]).astype(jnp.float32)
    reach = jnp.minimum(link + jnp.eye(DRAFT, dtype=jnp.float32), 1.0)
    for sweep in range((DRAFT - 1).bit_length()):
        reach = jnp.minimum(jnp.dot(reach, reach, precision=lax.Precision.HIGHEST), 1.0)
    depth = (jnp.sum(reach, axis=1) - 1.0).astype(jnp.int32)
    return (reach, depth)


def rotate(values, position):
    half = HD // 4
    freq = jnp.exp(jnp.arange(half, dtype=jnp.float32) * (-2.0 * math.log(10000.0) / (HD // 2)))
    angle = position.astype(jnp.float32)[..., None] * freq
    cosine = jnp.cos(angle)
    sine = jnp.sin(angle)
    first = values[..., :half]
    second = values[..., half : 2 * half]
    return jnp.concatenate(
        [first * cosine - second * sine, second * cosine + first * sine, values[..., 2 * half :]],
        axis=-1,
    )


def attend(queries, cache_keys, cache_values, tree_keys, tree_values, lengths, position, reach):
    window_span = cache_keys.shape[1]
    slot_ids = jnp.arange(window_span, dtype=jnp.int32)
    visible = (slot_ids[None, None, :] < lengths[:, None, None]) & (
        slot_ids[None, None, :] > position[:, :, None] - WINDOW
    )
    cache_scores = jnp.einsum(
        "rnhd,rcd->rhnc", queries, cache_keys, preferred_element_type=jnp.float32
    )
    tree_scores = jnp.einsum(
        "rnhd,rmd->rhnm", queries, tree_keys, preferred_element_type=jnp.float32
    )
    cache_scores = jnp.where(visible[:, None], cache_scores, -1e30)
    tree_scores = jnp.where(reach[:, None] > 0.5, tree_scores, -1e30)
    row_peak = jnp.maximum(jnp.max(cache_scores, axis=-1), jnp.max(tree_scores, axis=-1))[..., None]
    cache_weights = jnp.exp(cache_scores - row_peak)
    tree_weights = jnp.exp(tree_scores - row_peak)
    denominator = jnp.sum(cache_weights, axis=-1, keepdims=True) + jnp.sum(
        tree_weights, axis=-1, keepdims=True
    )
    cache_weights = (cache_weights / denominator).astype(jnp.bfloat16)
    tree_weights = (tree_weights / denominator).astype(jnp.bfloat16)
    result = jnp.einsum(
        "rhnc,rcd->rnhd", cache_weights, cache_values, preferred_element_type=jnp.float32
    )
    result = result + jnp.einsum(
        "rhnm,rmd->rnhd", tree_weights, tree_values, preferred_element_type=jnp.float32
    )
    return result.astype(jnp.bfloat16)


def refresh(logical_pages, length, leaf, reach, depth, new_keys, new_values):
    count = logical_pages.shape[0] * logical_pages.shape[2]
    logical = jnp.transpose(logical_pages, (1, 0, 2, 3)).reshape(2, count, HD)
    slot_ids = jnp.arange(count, dtype=jnp.int32)
    on_path = reach[leaf]
    selector = ((on_path[None, :] > 0.5) & (depth[None, :] == slot_ids[:, None] - length)).astype(
        jnp.float32
    )
    placed_keys = jnp.dot(selector, new_keys.astype(jnp.float32), precision=lax.Precision.HIGHEST)
    placed_values = jnp.dot(
        selector, new_values.astype(jnp.float32), precision=lax.Precision.HIGHEST
    )
    placed = jnp.stack([placed_keys, placed_values]).astype(jnp.bfloat16)
    written = jnp.sum(selector, axis=1) > 0.5
    logical = jnp.where(written[None, :, None], placed, logical)
    return jnp.transpose(
        logical.reshape(2, logical_pages.shape[0], logical_pages.shape[2], HD), (1, 0, 2, 3)
    )


def ring_gather(piece, axis):
    size = lax.axis_size(axis)
    if size == 1:
        return piece[None]
    index = lax.axis_index(axis)
    by_offset = {0: piece}
    ahead = piece
    behind = piece
    for step in range(1, size // 2 + 1):
        ahead = lax.ppermute(ahead, axis, [(i, (i + 1) % size) for i in range(size)])
        by_offset[size - step] = ahead
        if step <= (size - 1) // 2:
            behind = lax.ppermute(behind, axis, [(i, (i - 1) % size) for i in range(size)])
            by_offset[step] = behind
    placed = jnp.zeros((size,) + piece.shape, piece.dtype)
    for offset in range(size):
        placed = lax.dynamic_update_slice_in_dim(
            placed, by_offset[offset][None], (index + offset) % size, axis=0
        )
    return placed


def grid_gather(piece):
    lanes = 128
    inner = ring_gather(piece.reshape(-1, lanes), "tx")
    outer = ring_gather(inner.reshape(-1, lanes), "tz")
    return outer.reshape(-1, piece.shape[0])


def shards(
    tokens,
    query_weight,
    keyvalue_weight,
    output_weight,
    cache,
    page_table,
    parents,
    cache_len,
    accepted_leaf,
):
    head_count = lax.axis_size("head")
    head_index = lax.axis_index("head")
    tok_index = lax.axis_index("tz") * lax.axis_size("tx") + lax.axis_index("tx")
    requests = parents.shape[0]
    assert requests == head_count
    pages_dev = cache.shape[0]
    part_rows = query_weight.shape[0]
    q_cols = (HQ * HD) // head_count
    kv_cols = (2 * HD) // head_count
    out_cols = output_weight.shape[1]
    wq_piece = lax.dynamic_slice_in_dim(query_weight, head_index * q_cols, q_cols, axis=1)
    wkv_piece = lax.dynamic_slice_in_dim(keyvalue_weight, head_index * kv_cols, kv_cols, axis=1)
    flat = jnp.concatenate(
        [wq_piece.reshape(-1), wkv_piece.reshape(-1), output_weight.reshape(-1)]
    )
    stacked = grid_gather(flat)
    tok_count = stacked.shape[0]
    n_q = part_rows * q_cols
    n_kv = part_rows * kv_cols
    wq_cols = stacked[:, :n_q].reshape(tok_count * part_rows, q_cols)
    wkv_cols = stacked[:, n_q : n_q + n_kv].reshape(tok_count * part_rows, kv_cols)
    wo_cols = (
        stacked[:, n_q + n_kv :]
        .reshape(tok_count, HQ * HD, out_cols)
        .transpose(1, 0, 2)
        .reshape(HQ * HD, tok_count * out_cols)
    )
    gathered = lax.all_gather(tokens, "head", axis=1, tiled=True)
    wide = gathered.astype(jnp.float32)
    mean_square = jnp.mean(wide * wide, axis=1, keepdims=True)
    normed = (wide * lax.rsqrt(mean_square + 1e-06)).astype(jnp.bfloat16)
    q_part = jnp.dot(normed, wq_cols, preferred_element_type=jnp.float32)
    kv_part = jnp.dot(normed, wkv_cols, preferred_element_type=jnp.float32)
    both = jnp.concatenate([q_part, kv_part], axis=1)
    mine = lax.all_to_all(both, "head", 0, 1, tiled=True)
    mine = mine.reshape(DRAFT, head_count, q_cols + kv_cols)
    q_pre = mine[:, :, :q_cols].reshape(DRAFT, HQ, HD)
    kv_pre = mine[:, :, q_cols:].reshape(DRAFT, 2 * HD)
    parent_row = lax.dynamic_index_in_dim(parents, head_index, 0, keepdims=False)
    length = lax.dynamic_index_in_dim(cache_len, head_index, 0, keepdims=False)
    leaf = lax.dynamic_index_in_dim(accepted_leaf, head_index, 0, keepdims=False)
    reach, depth = ancestry(parent_row)
    position = length + depth
    queries = (rotate(q_pre, position[:, None]) * HD ** (-0.5)).astype(jnp.bfloat16)
    tree_keys = rotate(kv_pre[:, :HD], position).astype(jnp.bfloat16)
    tree_values = kv_pre[:, HD:].astype(jnp.bfloat16)
    device = tok_index * head_count + head_index
    own_table = (
        lax.dynamic_index_in_dim(page_table, head_index, 0, keepdims=False) - device * pages_dev
    )
    own_pages = jnp.take(cache, own_table, axis=0)
    cache_keys = own_pages[:, 0].reshape(NPR * PAGE, HD)
    cache_values = own_pages[:, 1].reshape(NPR * PAGE, HD)
    result = attend(
        queries[None],
        cache_keys[None],
        cache_values[None],
        tree_keys[None],
        tree_values[None],
        length[None],
        position[None],
        reach[None],
    )
    mixed = lax.all_gather(result.reshape(DRAFT, HQ * HD), "head", axis=0, tiled=True)
    summed = jnp.zeros((mixed.shape[0], wo_cols.shape[1]), jnp.float32)
    for group in range(head_count):
        head_ids = [k for k in range(group, HQ, head_count)]
        if not head_ids:
            continue
        partial_value = None
        for k in head_ids:
            term = jnp.dot(
                mixed[:, k * HD : (k + 1) * HD],
                wo_cols[k * HD : (k + 1) * HD],
                preferred_element_type=jnp.float32,
            )
            partial_value = term if partial_value is None else partial_value + term
        summed = summed + partial_value.astype(jnp.bfloat16).astype(jnp.float32)
    attended = summed.astype(jnp.bfloat16)
    new_pages = refresh(own_pages, length, leaf, reach, depth, tree_keys, tree_values)
    matches = (own_table[:, None] == jnp.arange(pages_dev, dtype=jnp.int32)[None, :]).astype(
        jnp.int32
    )
    inverse = jnp.sum(matches * jnp.arange(pages_dev, dtype=jnp.int32)[:, None], axis=0)
    cache_out = jnp.take(new_pages, inverse, axis=0)
    return (attended, cache_out)


def solution(mesh):
    tok_size = mesh.shape["tok"]
    tx_size = 4 if tok_size % 4 == 0 else tok_size
    grid = Mesh(
        mesh.devices.reshape(tok_size // tx_size, tx_size, mesh.shape["head"]),
        ("tz", "tx", "head"),
    )
    tok = ("tz", "tx")
    in_specs = (
        P(tok, "head"),
        P(tok, None),
        P(tok, None),
        P(None, ("head",) + tok),
        P(tok + ("head",), None, None, None),
        P(tok, None),
        P(tok, None),
        P(tok),
        P(tok),
    )
    out_specs = (P(tok, "head"), P(tok + ("head",), None, None, None))
    return jax.shard_map(shards, mesh=grid, in_specs=in_specs, out_specs=out_specs, check_vma=False)
```

```python
import math

import jax
import jax.numpy as jnp
from jax import lax
from jax.sharding import Mesh, PartitionSpec as P

HQ = 10
HD = 256
DRAFT = 64
PAGE = 128
NPR = 4
WINDOW = 256


def ancestry(parent_row):
    node_ids = jnp.arange(DRAFT, dtype=jnp.int32)
    link = (parent_row[:, None] == node_ids[None, :]).astype(jnp.float32)
    reach = jnp.minimum(link + jnp.eye(DRAFT, dtype=jnp.float32), 1.0)
    for sweep in range((DRAFT - 1).bit_length()):
        reach = jnp.minimum(jnp.dot(reach, reach, precision=lax.Precision.HIGHEST), 1.0)
    depth = (jnp.sum(reach, axis=1) - 1.0).astype(jnp.int32)
    return (reach, depth)


def rotate(values, position):
    half = HD // 4
    freq = jnp.exp(jnp.arange(half, dtype=jnp.float32) * (-2.0 * math.log(10000.0) / (HD // 2)))
    angle = position.astype(jnp.float32)[..., None] * freq
    cosine = jnp.cos(angle)
    sine = jnp.sin(angle)
    first = values[..., :half]
    second = values[..., half : 2 * half]
    return jnp.concatenate(
        [first * cosine - second * sine, second * cosine + first * sine, values[..., 2 * half :]],
        axis=-1,
    )


def attend(queries, cache_keys, cache_values, tree_keys, tree_values, lengths, position, reach):
    window_span = cache_keys.shape[1]
    slot_ids = jnp.arange(window_span, dtype=jnp.int32)
    visible = (slot_ids[None, None, :] < lengths[:, None, None]) & (
        slot_ids[None, None, :] > position[:, :, None] - WINDOW
    )
    cache_scores = jnp.einsum(
        "rnhd,rcd->rhnc", queries, cache_keys, preferred_element_type=jnp.float32
    )
    tree_scores = jnp.einsum(
        "rnhd,rmd->rhnm", queries, tree_keys, preferred_element_type=jnp.float32
    )
    cache_scores = jnp.where(visible[:, None], cache_scores, -1e30)
    tree_scores = jnp.where(reach[:, None] > 0.5, tree_scores, -1e30)
    row_peak = jnp.maximum(jnp.max(cache_scores, axis=-1), jnp.max(tree_scores, axis=-1))[..., None]
    cache_weights = jnp.exp(cache_scores - row_peak)
    tree_weights = jnp.exp(tree_scores - row_peak)
    denominator = jnp.sum(cache_weights, axis=-1, keepdims=True) + jnp.sum(
        tree_weights, axis=-1, keepdims=True
    )
    cache_weights = (cache_weights / denominator).astype(jnp.bfloat16)
    tree_weights = (tree_weights / denominator).astype(jnp.bfloat16)
    result = jnp.einsum(
        "rhnc,rcd->rnhd", cache_weights, cache_values, preferred_element_type=jnp.float32
    )
    result = result + jnp.einsum(
        "rhnm,rmd->rnhd", tree_weights, tree_values, preferred_element_type=jnp.float32
    )
    return result.astype(jnp.bfloat16)


def refresh(logical_pages, length, leaf, reach, depth, new_keys, new_values):
    count = logical_pages.shape[0] * logical_pages.shape[2]
    logical = jnp.transpose(logical_pages, (1, 0, 2, 3)).reshape(2, count, HD)
    slot_ids = jnp.arange(count, dtype=jnp.int32)
    on_path = reach[leaf]
    selector = ((on_path[None, :] > 0.5) & (depth[None, :] == slot_ids[:, None] - length)).astype(
        jnp.float32
    )
    placed_keys = jnp.dot(selector, new_keys.astype(jnp.float32), precision=lax.Precision.HIGHEST)
    placed_values = jnp.dot(
        selector, new_values.astype(jnp.float32), precision=lax.Precision.HIGHEST
    )
    placed = jnp.stack([placed_keys, placed_values]).astype(jnp.bfloat16)
    written = jnp.sum(selector, axis=1) > 0.5
    logical = jnp.where(written[None, :, None], placed, logical)
    return jnp.transpose(
        logical.reshape(2, logical_pages.shape[0], logical_pages.shape[2], HD), (1, 0, 2, 3)
    )


def ring_pieces(piece, axis):
    size = lax.axis_size(axis)
    by_offset = {0: piece}
    ahead = piece
    behind = piece
    for step in range(1, size // 2 + 1):
        ahead = lax.ppermute(ahead, axis, [(i, (i + 1) % size) for i in range(size)])
        by_offset[size - step] = ahead
        if step <= (size - 1) // 2:
            behind = lax.ppermute(behind, axis, [(i, (i - 1) % size) for i in range(size)])
            by_offset[step] = behind
    return by_offset


def grid_gather(piece):
    z_size = lax.axis_size("tz")
    x_size = lax.axis_size("tx")
    z_index = lax.axis_index("tz")
    x_index = lax.axis_index("tx")
    column = jnp.zeros((z_size,) + piece.shape, piece.dtype)
    for offset, got in ring_pieces(piece, "tz").items():
        column = lax.dynamic_update_slice_in_dim(
            column, got[None], (z_index + offset) % z_size, axis=0
        )
    placed = jnp.zeros((z_size, x_size) + piece.shape, piece.dtype)
    for offset, got in ring_pieces(column, "tx").items():
        placed = lax.dynamic_update_slice_in_dim(
            placed, got[:, None], (x_index + offset) % x_size, axis=1
        )
    return placed.reshape((z_size * x_size,) + piece.shape)


def shards(
    tokens,
    query_weight,
    keyvalue_weight,
    output_weight,
    cache,
    page_table,
    parents,
    cache_len,
    accepted_leaf,
):
    head_count = lax.axis_size("head")
    head_index = lax.axis_index("head")
    tok_index = lax.axis_index("tz") * lax.axis_size("tx") + lax.axis_index("tx")
    requests = parents.shape[0]
    assert requests == head_count
    pages_dev = cache.shape[0]
    part_rows = query_weight.shape[0]
    q_cols = (HQ * HD) // head_count
    kv_cols = (2 * HD) // head_count
    out_cols = output_weight.shape[1]
    wq_piece = lax.dynamic_slice_in_dim(query_weight, head_index * q_cols, q_cols, axis=1)
    wkv_piece = lax.dynamic_slice_in_dim(keyvalue_weight, head_index * kv_cols, kv_cols, axis=1)
    proj_piece = jnp.concatenate([wq_piece, wkv_piece], axis=1)
    width = proj_piece.shape[1]
    wo_flat = output_weight.reshape(-1)
    wo_rows = -(-wo_flat.shape[0] // width)
    wo_rows = -(-(part_rows + wo_rows) // 8) * 8 - part_rows
    wo_block = jnp.pad(wo_flat, (0, wo_rows * width - wo_flat.shape[0])).reshape(wo_rows, width)
    piece = jnp.concatenate([proj_piece, wo_block], axis=0)
    stacked = grid_gather(piece)
    tok_count = stacked.shape[0]
    proj_w = stacked[:, :part_rows].reshape(tok_count * part_rows, width)
    wo_cols = (
        stacked[:, part_rows:]
        .reshape(tok_count, -1)[:, : wo_flat.shape[0]]
        .reshape(tok_count, HQ * HD, out_cols)
        .transpose(1, 0, 2)
        .reshape(HQ * HD, tok_count * out_cols)
    )
    gathered = lax.all_gather(tokens, "head", axis=1, tiled=True)
    wide = gathered.astype(jnp.float32)
    mean_square = jnp.mean(wide * wide, axis=1, keepdims=True)
    normed = (wide * lax.rsqrt(mean_square + 1e-06)).astype(jnp.bfloat16)
    both = jnp.dot(normed, proj_w, preferred_element_type=jnp.float32)
    mine = lax.all_to_all(both, "head", 0, 1, tiled=True)
    mine = mine.reshape(DRAFT, head_count, q_cols + kv_cols)
    q_pre = mine[:, :, :q_cols].reshape(DRAFT, HQ, HD)
    kv_pre = mine[:, :, q_cols:].reshape(DRAFT, 2 * HD)
    parent_row = lax.dynamic_index_in_dim(parents, head_index, 0, keepdims=False)
    length = lax.dynamic_index_in_dim(cache_len, head_index, 0, keepdims=False)
    leaf = lax.dynamic_index_in_dim(accepted_leaf, head_index, 0, keepdims=False)
    reach, depth = ancestry(parent_row)
    position = length + depth
    queries = (rotate(q_pre, position[:, None]) * HD ** (-0.5)).astype(jnp.bfloat16)
    tree_keys = rotate(kv_pre[:, :HD], position).astype(jnp.bfloat16)
    tree_values = kv_pre[:, HD:].astype(jnp.bfloat16)
    device = tok_index * head_count + head_index
    own_table = (
        lax.dynamic_index_in_dim(page_table, head_index, 0, keepdims=False) - device * pages_dev
    )
    own_pages = jnp.take(cache, own_table, axis=0)
    cache_keys = own_pages[:, 0].reshape(NPR * PAGE, HD)
    cache_values = own_pages[:, 1].reshape(NPR * PAGE, HD)
    result = attend(
        queries[None],
        cache_keys[None],
        cache_values[None],
        tree_keys[None],
        tree_values[None],
        length[None],
        position[None],
        reach[None],
    )
    mixed = lax.all_gather(result.reshape(DRAFT, HQ * HD), "head", axis=0, tiled=True)
    summed = jnp.zeros((mixed.shape[0], wo_cols.shape[1]), jnp.float32)
    for group in range(head_count):
        head_ids = [k for k in range(group, HQ, head_count)]
        if not head_ids:
            continue
        partial_value = None
        for k in head_ids:
            term = jnp.dot(
                mixed[:, k * HD : (k + 1) * HD],
                wo_cols[k * HD : (k + 1) * HD],
                preferred_element_type=jnp.float32,
            )
            partial_value = term if partial_value is None else partial_value + term
        summed = summed + partial_value.astype(jnp.bfloat16).astype(jnp.float32)
    attended = summed.astype(jnp.bfloat16)
    new_pages = refresh(own_pages, length, leaf, reach, depth, tree_keys, tree_values)
    matches = (own_table[:, None] == jnp.arange(pages_dev, dtype=jnp.int32)[None, :]).astype(
        jnp.int32
    )
    inverse = jnp.sum(matches * jnp.arange(pages_dev, dtype=jnp.int32)[:, None], axis=0)
    cache_out = jnp.take(new_pages, inverse, axis=0)
    return (attended, cache_out)


def solution(mesh):
    tok_size = mesh.shape["tok"]
    tx_size = 4 if tok_size % 4 == 0 else tok_size
    grid = Mesh(
        mesh.devices.reshape(tok_size // tx_size, tx_size, mesh.shape["head"]),
        ("tz", "tx", "head"),
    )
    tok = ("tz", "tx")
    in_specs = (
        P(tok, "head"),
        P(tok, None),
        P(tok, None),
        P(None, ("head",) + tok),
        P(tok + ("head",), None, None, None),
        P(tok, None),
        P(tok, None),
        P(tok),
        P(tok),
    )
    out_specs = (P(tok, "head"), P(tok + ("head",), None, None, None))
    return jax.shard_map(shards, mesh=grid, in_specs=in_specs, out_specs=out_specs, check_vma=False)
```

```python
import math

import jax
import jax.numpy as jnp
from jax import lax
from jax.sharding import Mesh, PartitionSpec as P

HQ = 10
HD = 256
DRAFT = 64
PAGE = 128
NPR = 4
WINDOW = 256


def ancestry(parent_row):
    node_ids = jnp.arange(DRAFT, dtype=jnp.int32)
    link = (parent_row[:, None] == node_ids[None, :]).astype(jnp.float32)
    reach = jnp.minimum(link + jnp.eye(DRAFT, dtype=jnp.float32), 1.0)
    for sweep in range((DRAFT - 1).bit_length()):
        reach = jnp.minimum(jnp.dot(reach, reach, precision=lax.Precision.HIGHEST), 1.0)
    depth = (jnp.sum(reach, axis=1) - 1.0).astype(jnp.int32)
    return (reach, depth)


def rotate(values, position):
    half = HD // 4
    freq = jnp.exp(jnp.arange(half, dtype=jnp.float32) * (-2.0 * math.log(10000.0) / (HD // 2)))
    angle = position.astype(jnp.float32)[..., None] * freq
    cosine = jnp.cos(angle)
    sine = jnp.sin(angle)
    first = values[..., :half]
    second = values[..., half : 2 * half]
    return jnp.concatenate(
        [first * cosine - second * sine, second * cosine + first * sine, values[..., 2 * half :]],
        axis=-1,
    )


def attend(queries, cache_keys, cache_values, tree_keys, tree_values, lengths, position, reach):
    window_span = cache_keys.shape[1]
    slot_ids = jnp.arange(window_span, dtype=jnp.int32)
    visible = (slot_ids[None, None, :] < lengths[:, None, None]) & (
        slot_ids[None, None, :] > position[:, :, None] - WINDOW
    )
    cache_scores = jnp.einsum(
        "rnhd,rcd->rhnc", queries, cache_keys, preferred_element_type=jnp.float32
    )
    tree_scores = jnp.einsum(
        "rnhd,rmd->rhnm", queries, tree_keys, preferred_element_type=jnp.float32
    )
    cache_scores = jnp.where(visible[:, None], cache_scores, -1e30)
    tree_scores = jnp.where(reach[:, None] > 0.5, tree_scores, -1e30)
    row_peak = jnp.maximum(jnp.max(cache_scores, axis=-1), jnp.max(tree_scores, axis=-1))[..., None]
    cache_weights = jnp.exp(cache_scores - row_peak)
    tree_weights = jnp.exp(tree_scores - row_peak)
    denominator = jnp.sum(cache_weights, axis=-1, keepdims=True) + jnp.sum(
        tree_weights, axis=-1, keepdims=True
    )
    cache_weights = (cache_weights / denominator).astype(jnp.bfloat16)
    tree_weights = (tree_weights / denominator).astype(jnp.bfloat16)
    result = jnp.einsum(
        "rhnc,rcd->rnhd", cache_weights, cache_values, preferred_element_type=jnp.float32
    )
    result = result + jnp.einsum(
        "rhnm,rmd->rnhd", tree_weights, tree_values, preferred_element_type=jnp.float32
    )
    return result.astype(jnp.bfloat16)


def refresh(logical_pages, length, leaf, reach, depth, new_keys, new_values):
    count = logical_pages.shape[0] * logical_pages.shape[2]
    logical = jnp.transpose(logical_pages, (1, 0, 2, 3)).reshape(2, count, HD)
    slot_ids = jnp.arange(count, dtype=jnp.int32)
    on_path = reach[leaf]
    selector = ((on_path[None, :] > 0.5) & (depth[None, :] == slot_ids[:, None] - length)).astype(
        jnp.float32
    )
    placed_keys = jnp.dot(selector, new_keys.astype(jnp.float32), precision=lax.Precision.HIGHEST)
    placed_values = jnp.dot(
        selector, new_values.astype(jnp.float32), precision=lax.Precision.HIGHEST
    )
    placed = jnp.stack([placed_keys, placed_values]).astype(jnp.bfloat16)
    written = jnp.sum(selector, axis=1) > 0.5
    logical = jnp.where(written[None, :, None], placed, logical)
    return jnp.transpose(
        logical.reshape(2, logical_pages.shape[0], logical_pages.shape[2], HD), (1, 0, 2, 3)
    )


def ring_pieces(piece, axis):
    size = lax.axis_size(axis)
    by_offset = {0: piece}
    ahead = piece
    behind = piece
    for step in range(1, size // 2 + 1):
        ahead = lax.ppermute(ahead, axis, [(i, (i + 1) % size) for i in range(size)])
        by_offset[size - step] = ahead
        if step <= (size - 1) // 2:
            behind = lax.ppermute(behind, axis, [(i, (i - 1) % size) for i in range(size)])
            by_offset[step] = behind
    return by_offset


def grid_gather(piece):
    z_size = lax.axis_size("tz")
    x_size = lax.axis_size("tx")
    z_index = lax.axis_index("tz")
    x_index = lax.axis_index("tx")
    column = jnp.zeros((z_size,) + piece.shape, piece.dtype)
    for offset, got in ring_pieces(piece, "tz").items():
        column = lax.dynamic_update_slice_in_dim(
            column, got[None], (z_index + offset) % z_size, axis=0
        )
    placed = lax.all_gather(column, "tx", axis=1, tiled=False)
    return placed.reshape((z_size * x_size,) + piece.shape)


def shards(
    tokens,
    query_weight,
    keyvalue_weight,
    output_weight,
    cache,
    page_table,
    parents,
    cache_len,
    accepted_leaf,
):
    head_count = lax.axis_size("head")
    head_index = lax.axis_index("head")
    tok_index = lax.axis_index("tz") * lax.axis_size("tx") + lax.axis_index("tx")
    requests = parents.shape[0]
    assert requests == head_count
    pages_dev = cache.shape[0]
    part_rows = query_weight.shape[0]
    q_cols = (HQ * HD) // head_count
    kv_cols = (2 * HD) // head_count
    out_cols = output_weight.shape[1]
    wq_piece = lax.dynamic_slice_in_dim(query_weight, head_index * q_cols, q_cols, axis=1)
    wkv_piece = lax.dynamic_slice_in_dim(keyvalue_weight, head_index * kv_cols, kv_cols, axis=1)
    proj_piece = jnp.concatenate([wq_piece, wkv_piece], axis=1)
    width = proj_piece.shape[1]
    wo_flat = output_weight.reshape(-1)
    wo_rows = -(-wo_flat.shape[0] // width)
    wo_rows = -(-(part_rows + wo_rows) // 8) * 8 - part_rows
    wo_block = jnp.pad(wo_flat, (0, wo_rows * width - wo_flat.shape[0])).reshape(wo_rows, width)
    piece = jnp.concatenate([proj_piece, wo_block], axis=0)
    stacked = grid_gather(piece)
    tok_count = stacked.shape[0]
    proj_w = stacked[:, :part_rows].reshape(tok_count * part_rows, width)
    wo_cols = (
        stacked[:, part_rows:]
        .reshape(tok_count, -1)[:, : wo_flat.shape[0]]
        .reshape(tok_count, HQ * HD, out_cols)
        .transpose(1, 0, 2)
        .reshape(HQ * HD, tok_count * out_cols)
    )
    gathered = lax.all_gather(tokens, "head", axis=1, tiled=True)
    wide = gathered.astype(jnp.float32)
    mean_square = jnp.mean(wide * wide, axis=1, keepdims=True)
    normed = (wide * lax.rsqrt(mean_square + 1e-06)).astype(jnp.bfloat16)
    both = jnp.dot(normed, proj_w, preferred_element_type=jnp.float32)
    mine = lax.all_to_all(both, "head", 0, 1, tiled=True)
    mine = mine.reshape(DRAFT, head_count, q_cols + kv_cols)
    q_pre = mine[:, :, :q_cols].reshape(DRAFT, HQ, HD)
    kv_pre = mine[:, :, q_cols:].reshape(DRAFT, 2 * HD)
    parent_row = lax.dynamic_index_in_dim(parents, head_index, 0, keepdims=False)
    length = lax.dynamic_index_in_dim(cache_len, head_index, 0, keepdims=False)
    leaf = lax.dynamic_index_in_dim(accepted_leaf, head_index, 0, keepdims=False)
    reach, depth = ancestry(parent_row)
    position = length + depth
    queries = (rotate(q_pre, position[:, None]) * HD ** (-0.5)).astype(jnp.bfloat16)
    tree_keys = rotate(kv_pre[:, :HD], position).astype(jnp.bfloat16)
    tree_values = kv_pre[:, HD:].astype(jnp.bfloat16)
    device = tok_index * head_count + head_index
    own_table = (
        lax.dynamic_index_in_dim(page_table, head_index, 0, keepdims=False) - device * pages_dev
    )
    own_pages = jnp.take(cache, own_table, axis=0)
    cache_keys = own_pages[:, 0].reshape(NPR * PAGE, HD)
    cache_values = own_pages[:, 1].reshape(NPR * PAGE, HD)
    result = attend(
        queries[None],
        cache_keys[None],
        cache_values[None],
        tree_keys[None],
        tree_values[None],
        length[None],
        position[None],
        reach[None],
    )
    mixed = lax.all_gather(result.reshape(DRAFT, HQ * HD), "head", axis=0, tiled=True)
    per_head = lax.dot_general(
        mixed.reshape(mixed.shape[0], HQ, HD),
        wo_cols.reshape(HQ, HD, wo_cols.shape[1]),
        (((2,), (1,)), ((1,), (0,))),
        preferred_element_type=jnp.float32,
    )
    summed = None
    for group in range(head_count):
        head_ids = [k for k in range(group, HQ, head_count)]
        if not head_ids:
            continue
        partial_value = per_head[head_ids[0]]
        for k in head_ids[1:]:
            partial_value = partial_value + per_head[k]
        term = partial_value.astype(jnp.bfloat16).astype(jnp.float32)
        summed = term if summed is None else summed + term
    attended = summed.astype(jnp.bfloat16)
    new_pages = refresh(own_pages, length, leaf, reach, depth, tree_keys, tree_values)
    matches = (own_table[:, None] == jnp.arange(pages_dev, dtype=jnp.int32)[None, :]).astype(
        jnp.int32
    )
    inverse = jnp.sum(matches * jnp.arange(pages_dev, dtype=jnp.int32)[:, None], axis=0)
    cache_out = jnp.take(new_pages, inverse, axis=0)
    return (attended, cache_out)


def solution(mesh):
    tok_size = mesh.shape["tok"]
    tx_size = 4 if tok_size % 4 == 0 else tok_size
    grid = Mesh(
        mesh.devices.reshape(tok_size // tx_size, tx_size, mesh.shape["head"]),
        ("tz", "tx", "head"),
    )
    tok = ("tz", "tx")
    in_specs = (
        P(tok, "head"),
        P(tok, None),
        P(tok, None),
        P(None, ("head",) + tok),
        P(tok + ("head",), None, None, None),
        P(tok, None),
        P(tok, None),
        P(tok),
        P(tok),
    )
    out_specs = (P(tok, "head"), P(tok + ("head",), None, None, None))
    return jax.shard_map(shards, mesh=grid, in_specs=in_specs, out_specs=out_specs, check_vma=False)
```

```python
import math

import jax
import jax.numpy as jnp
from jax import lax
from jax.sharding import Mesh, PartitionSpec as P

HQ = 10
HD = 256
DRAFT = 64
PAGE = 128
NPR = 4
WINDOW = 256


def ancestry(parent_row):
    node_ids = jnp.arange(DRAFT, dtype=jnp.int32)
    link = (parent_row[:, None] == node_ids[None, :]).astype(jnp.float32)
    reach = jnp.minimum(link + jnp.eye(DRAFT, dtype=jnp.float32), 1.0)
    for sweep in range((DRAFT - 1).bit_length()):
        reach = jnp.minimum(jnp.dot(reach, reach, precision=lax.Precision.HIGHEST), 1.0)
    depth = (jnp.sum(reach, axis=1) - 1.0).astype(jnp.int32)
    return (reach, depth)


def rotate(values, position):
    half = HD // 4
    freq = jnp.exp(jnp.arange(half, dtype=jnp.float32) * (-2.0 * math.log(10000.0) / (HD // 2)))
    angle = position.astype(jnp.float32)[..., None] * freq
    cosine = jnp.cos(angle)
    sine = jnp.sin(angle)
    first = values[..., :half]
    second = values[..., half : 2 * half]
    return jnp.concatenate(
        [first * cosine - second * sine, second * cosine + first * sine, values[..., 2 * half :]],
        axis=-1,
    )


def attend(queries, cache_keys, cache_values, tree_keys, tree_values, lengths, position, reach):
    window_span = cache_keys.shape[1]
    slot_ids = jnp.arange(window_span, dtype=jnp.int32)
    visible = (slot_ids[None, None, :] < lengths[:, None, None]) & (
        slot_ids[None, None, :] > position[:, :, None] - WINDOW
    )
    cache_scores = jnp.einsum(
        "rnhd,rcd->rhnc", queries, cache_keys, preferred_element_type=jnp.float32
    )
    tree_scores = jnp.einsum(
        "rnhd,rmd->rhnm", queries, tree_keys, preferred_element_type=jnp.float32
    )
    cache_scores = jnp.where(visible[:, None], cache_scores, -1e30)
    tree_scores = jnp.where(reach[:, None] > 0.5, tree_scores, -1e30)
    row_peak = jnp.maximum(jnp.max(cache_scores, axis=-1), jnp.max(tree_scores, axis=-1))[..., None]
    cache_weights = jnp.exp(cache_scores - row_peak)
    tree_weights = jnp.exp(tree_scores - row_peak)
    denominator = jnp.sum(cache_weights, axis=-1, keepdims=True) + jnp.sum(
        tree_weights, axis=-1, keepdims=True
    )
    cache_weights = (cache_weights / denominator).astype(jnp.bfloat16)
    tree_weights = (tree_weights / denominator).astype(jnp.bfloat16)
    result = jnp.einsum(
        "rhnc,rcd->rnhd", cache_weights, cache_values, preferred_element_type=jnp.float32
    )
    result = result + jnp.einsum(
        "rhnm,rmd->rnhd", tree_weights, tree_values, preferred_element_type=jnp.float32
    )
    return result.astype(jnp.bfloat16)


def refresh(logical_pages, length, leaf, reach, depth, new_keys, new_values):
    count = logical_pages.shape[0] * logical_pages.shape[2]
    logical = jnp.transpose(logical_pages, (1, 0, 2, 3)).reshape(2, count, HD)
    slot_ids = jnp.arange(count, dtype=jnp.int32)
    on_path = reach[leaf]
    selector = ((on_path[None, :] > 0.5) & (depth[None, :] == slot_ids[:, None] - length)).astype(
        jnp.float32
    )
    placed_keys = jnp.dot(selector, new_keys.astype(jnp.float32), precision=lax.Precision.HIGHEST)
    placed_values = jnp.dot(
        selector, new_values.astype(jnp.float32), precision=lax.Precision.HIGHEST
    )
    placed = jnp.stack([placed_keys, placed_values]).astype(jnp.bfloat16)
    written = jnp.sum(selector, axis=1) > 0.5
    logical = jnp.where(written[None, :, None], placed, logical)
    return jnp.transpose(
        logical.reshape(2, logical_pages.shape[0], logical_pages.shape[2], HD), (1, 0, 2, 3)
    )


def ring_pieces(piece, axis):
    size = lax.axis_size(axis)
    got = [(0, 0, piece)]
    ahead = piece
    behind = piece
    forward = [(i, (i + 1) % size) for i in range(size)]
    backward = [(i, (i - 1) % size) for i in range(size)]
    for step in range(1, size // 2 + 1):
        if 2 * step == size and size > 2:
            half = piece.shape[0] // 2
            got.append((step, 0, lax.ppermute(ahead[:half], axis, forward)))
            got.append((step, half, lax.ppermute(behind[half:], axis, backward)))
            break
        ahead = lax.ppermute(ahead, axis, forward)
        got.append((size - step, 0, ahead))
        if step <= (size - 1) // 2:
            behind = lax.ppermute(behind, axis, backward)
            got.append((step, 0, behind))
    return got


def grid_gather(piece):
    z_size = lax.axis_size("tz")
    x_size = lax.axis_size("tx")
    z_index = lax.axis_index("tz")
    x_index = lax.axis_index("tx")
    zero = jnp.int32(0)
    column = jnp.zeros((z_size,) + piece.shape, piece.dtype)
    for offset, first, part in ring_pieces(piece, "tz"):
        column = lax.dynamic_update_slice(
            column, part[None], ((z_index + offset) % z_size, jnp.int32(first), zero)
        )
    placed = jnp.zeros((z_size, x_size) + piece.shape, piece.dtype)
    for offset, first, part in ring_pieces(column, "tx"):
        placed = lax.dynamic_update_slice(
            placed, part[:, None], (jnp.int32(first), (x_index + offset) % x_size, zero, zero)
        )
    return placed.reshape((z_size * x_size,) + piece.shape)


def shards(
    tokens,
    query_weight,
    keyvalue_weight,
    output_weight,
    cache,
    page_table,
    parents,
    cache_len,
    accepted_leaf,
):
    head_count = lax.axis_size("head")
    head_index = lax.axis_index("head")
    tok_index = lax.axis_index("tz") * lax.axis_size("tx") + lax.axis_index("tx")
    requests = parents.shape[0]
    assert requests == head_count
    pages_dev = cache.shape[0]
    part_rows = query_weight.shape[0]
    q_cols = (HQ * HD) // head_count
    kv_cols = (2 * HD) // head_count
    out_cols = output_weight.shape[1]
    wq_piece = lax.dynamic_slice_in_dim(query_weight, head_index * q_cols, q_cols, axis=1)
    wkv_piece = lax.dynamic_slice_in_dim(keyvalue_weight, head_index * kv_cols, kv_cols, axis=1)
    proj_piece = jnp.concatenate([wq_piece, wkv_piece], axis=1)
    width = proj_piece.shape[1]
    wo_flat = output_weight.reshape(-1)
    wo_rows = -(-wo_flat.shape[0] // width)
    wo_rows = -(-(part_rows + wo_rows) // 8) * 8 - part_rows
    wo_block = jnp.pad(wo_flat, (0, wo_rows * width - wo_flat.shape[0])).reshape(wo_rows, width)
    piece = jnp.concatenate([proj_piece, wo_block], axis=0)
    stacked = grid_gather(piece)
    tok_count = stacked.shape[0]
    proj_w = stacked[:, :part_rows].reshape(tok_count * part_rows, width)
    wo_cols = (
        stacked[:, part_rows:]
        .reshape(tok_count, -1)[:, : wo_flat.shape[0]]
        .reshape(tok_count, HQ * HD, out_cols)
        .transpose(1, 0, 2)
        .reshape(HQ * HD, tok_count * out_cols)
    )
    gathered = lax.all_gather(tokens, "head", axis=1, tiled=True)
    wide = gathered.astype(jnp.float32)
    mean_square = jnp.mean(wide * wide, axis=1, keepdims=True)
    normed = (wide * lax.rsqrt(mean_square + 1e-06)).astype(jnp.bfloat16)
    both = jnp.dot(normed, proj_w, preferred_element_type=jnp.float32)
    mine = lax.all_to_all(both, "head", 0, 1, tiled=True)
    mine = mine.reshape(DRAFT, head_count, q_cols + kv_cols)
    q_pre = mine[:, :, :q_cols].reshape(DRAFT, HQ, HD)
    kv_pre = mine[:, :, q_cols:].reshape(DRAFT, 2 * HD)
    parent_row = lax.dynamic_index_in_dim(parents, head_index, 0, keepdims=False)
    length = lax.dynamic_index_in_dim(cache_len, head_index, 0, keepdims=False)
    leaf = lax.dynamic_index_in_dim(accepted_leaf, head_index, 0, keepdims=False)
    reach, depth = ancestry(parent_row)
    position = length + depth
    queries = (rotate(q_pre, position[:, None]) * HD ** (-0.5)).astype(jnp.bfloat16)
    tree_keys = rotate(kv_pre[:, :HD], position).astype(jnp.bfloat16)
    tree_values = kv_pre[:, HD:].astype(jnp.bfloat16)
    device = tok_index * head_count + head_index
    own_table = (
        lax.dynamic_index_in_dim(page_table, head_index, 0, keepdims=False) - device * pages_dev
    )
    own_pages = jnp.take(cache, own_table, axis=0)
    cache_keys = own_pages[:, 0].reshape(NPR * PAGE, HD)
    cache_values = own_pages[:, 1].reshape(NPR * PAGE, HD)
    result = attend(
        queries[None],
        cache_keys[None],
        cache_values[None],
        tree_keys[None],
        tree_values[None],
        length[None],
        position[None],
        reach[None],
    )
    mixed = lax.all_gather(result.reshape(DRAFT, HQ * HD), "head", axis=0, tiled=True)
    per_head = lax.dot_general(
        mixed.reshape(mixed.shape[0], HQ, HD),
        wo_cols.reshape(HQ, HD, wo_cols.shape[1]),
        (((2,), (1,)), ((1,), (0,))),
        preferred_element_type=jnp.float32,
    )
    summed = None
    for group in range(head_count):
        head_ids = [k for k in range(group, HQ, head_count)]
        if not head_ids:
            continue
        partial_value = per_head[head_ids[0]]
        for k in head_ids[1:]:
            partial_value = partial_value + per_head[k]
        term = partial_value.astype(jnp.bfloat16).astype(jnp.float32)
        summed = term if summed is None else summed + term
    attended = summed.astype(jnp.bfloat16)
    new_pages = refresh(own_pages, length, leaf, reach, depth, tree_keys, tree_values)
    matches = (own_table[:, None] == jnp.arange(pages_dev, dtype=jnp.int32)[None, :]).astype(
        jnp.int32
    )
    inverse = jnp.sum(matches * jnp.arange(pages_dev, dtype=jnp.int32)[:, None], axis=0)
    cache_out = jnp.take(new_pages, inverse, axis=0)
    return (attended, cache_out)


def solution(mesh):
    tok_size = mesh.shape["tok"]
    tx_size = 4 if tok_size % 4 == 0 else tok_size
    grid = Mesh(
        mesh.devices.reshape(tok_size // tx_size, tx_size, mesh.shape["head"]),
        ("tz", "tx", "head"),
    )
    tok = ("tz", "tx")
    in_specs = (
        P(tok, "head"),
        P(tok, None),
        P(tok, None),
        P(None, ("head",) + tok),
        P(tok + ("head",), None, None, None),
        P(tok, None),
        P(tok, None),
        P(tok),
        P(tok),
    )
    out_specs = (P(tok, "head"), P(tok + ("head",), None, None, None))
    return jax.shard_map(shards, mesh=grid, in_specs=in_specs, out_specs=out_specs, check_vma=False)
```

```python
import math

import jax
import jax.numpy as jnp
from jax import lax
from jax.sharding import Mesh, PartitionSpec as P

HQ = 10
HD = 256
DRAFT = 64
PAGE = 128
NPR = 4
WINDOW = 256


def ancestry(parent_row):
    node_ids = jnp.arange(DRAFT, dtype=jnp.int32)
    link = (parent_row[:, None] == node_ids[None, :]).astype(jnp.float32)
    reach = jnp.minimum(link + jnp.eye(DRAFT, dtype=jnp.float32), 1.0)
    for sweep in range((DRAFT - 1).bit_length()):
        reach = jnp.minimum(jnp.dot(reach, reach, precision=lax.Precision.HIGHEST), 1.0)
    depth = (jnp.sum(reach, axis=1) - 1.0).astype(jnp.int32)
    return (reach, depth)


def rotate(values, position):
    half = HD // 4
    freq = jnp.exp(jnp.arange(half, dtype=jnp.float32) * (-2.0 * math.log(10000.0) / (HD // 2)))
    angle = position.astype(jnp.float32)[..., None] * freq
    cosine = jnp.cos(angle)
    sine = jnp.sin(angle)
    first = values[..., :half]
    second = values[..., half : 2 * half]
    return jnp.concatenate(
        [first * cosine - second * sine, second * cosine + first * sine, values[..., 2 * half :]],
        axis=-1,
    )


def attend(queries, cache_keys, cache_values, tree_keys, tree_values, lengths, position, reach):
    window_span = cache_keys.shape[1]
    slot_ids = jnp.arange(window_span, dtype=jnp.int32)
    visible = (slot_ids[None, None, :] < lengths[:, None, None]) & (
        slot_ids[None, None, :] > position[:, :, None] - WINDOW
    )
    cache_scores = jnp.einsum(
        "rnhd,rcd->rhnc", queries, cache_keys, preferred_element_type=jnp.float32
    )
    tree_scores = jnp.einsum(
        "rnhd,rmd->rhnm", queries, tree_keys, preferred_element_type=jnp.float32
    )
    cache_scores = jnp.where(visible[:, None], cache_scores, -1e30)
    tree_scores = jnp.where(reach[:, None] > 0.5, tree_scores, -1e30)
    row_peak = jnp.maximum(jnp.max(cache_scores, axis=-1), jnp.max(tree_scores, axis=-1))[..., None]
    cache_weights = jnp.exp(cache_scores - row_peak)
    tree_weights = jnp.exp(tree_scores - row_peak)
    denominator = jnp.sum(cache_weights, axis=-1, keepdims=True) + jnp.sum(
        tree_weights, axis=-1, keepdims=True
    )
    cache_weights = (cache_weights / denominator).astype(jnp.bfloat16)
    tree_weights = (tree_weights / denominator).astype(jnp.bfloat16)
    result = jnp.einsum(
        "rhnc,rcd->rnhd", cache_weights, cache_values, preferred_element_type=jnp.float32
    )
    result = result + jnp.einsum(
        "rhnm,rmd->rnhd", tree_weights, tree_values, preferred_element_type=jnp.float32
    )
    return result.astype(jnp.bfloat16)


def refresh(logical_pages, length, leaf, reach, depth, new_keys, new_values):
    count = logical_pages.shape[0] * logical_pages.shape[2]
    logical = jnp.transpose(logical_pages, (1, 0, 2, 3)).reshape(2, count, HD)
    slot_ids = jnp.arange(count, dtype=jnp.int32)
    on_path = reach[leaf]
    selector = ((on_path[None, :] > 0.5) & (depth[None, :] == slot_ids[:, None] - length)).astype(
        jnp.float32
    )
    placed_keys = jnp.dot(selector, new_keys.astype(jnp.float32), precision=lax.Precision.HIGHEST)
    placed_values = jnp.dot(
        selector, new_values.astype(jnp.float32), precision=lax.Precision.HIGHEST
    )
    placed = jnp.stack([placed_keys, placed_values]).astype(jnp.bfloat16)
    written = jnp.sum(selector, axis=1) > 0.5
    logical = jnp.where(written[None, :, None], placed, logical)
    return jnp.transpose(
        logical.reshape(2, logical_pages.shape[0], logical_pages.shape[2], HD), (1, 0, 2, 3)
    )


def ring_pieces(piece, axis):
    size = lax.axis_size(axis)
    got = [(0, 0, piece)]
    ahead = piece
    behind = piece
    forward = [(i, (i + 1) % size) for i in range(size)]
    backward = [(i, (i - 1) % size) for i in range(size)]
    for step in range(1, size // 2 + 1):
        if 2 * step == size and size > 2:
            half = piece.shape[0] // 2
            got.append((step, 0, lax.ppermute(ahead[:half], axis, forward)))
            got.append((step, half, lax.ppermute(behind[half:], axis, backward)))
            break
        ahead = lax.ppermute(ahead, axis, forward)
        got.append((size - step, 0, ahead))
        if step <= (size - 1) // 2:
            behind = lax.ppermute(behind, axis, backward)
            got.append((step, 0, behind))
    return got


def grid_gather(piece):
    z_size = lax.axis_size("tz")
    x_size = lax.axis_size("tx")
    z_index = lax.axis_index("tz")
    x_index = lax.axis_index("tx")
    zero = jnp.int32(0)
    column = jnp.zeros((z_size,) + piece.shape, piece.dtype)
    direct = [(0, 0, piece)] + [
        (k, 0, lax.ppermute(piece, "tz", [(i, (i - k) % z_size) for i in range(z_size)]))
        for k in range(1, z_size)
    ]
    for offset, first, part in direct:
        column = lax.dynamic_update_slice(
            column, part[None], ((z_index + offset) % z_size, jnp.int32(first), zero)
        )
    placed = jnp.zeros((z_size, x_size) + piece.shape, piece.dtype)
    for offset, first, part in ring_pieces(column, "tx"):
        placed = lax.dynamic_update_slice(
            placed, part[:, None], (jnp.int32(first), (x_index + offset) % x_size, zero, zero)
        )
    return placed.reshape((z_size * x_size,) + piece.shape)


def shards(
    tokens,
    query_weight,
    keyvalue_weight,
    output_weight,
    cache,
    page_table,
    parents,
    cache_len,
    accepted_leaf,
):
    head_count = lax.axis_size("head")
    head_index = lax.axis_index("head")
    tok_index = lax.axis_index("tz") * lax.axis_size("tx") + lax.axis_index("tx")
    requests = parents.shape[0]
    assert requests == head_count
    pages_dev = cache.shape[0]
    part_rows = query_weight.shape[0]
    q_cols = (HQ * HD) // head_count
    kv_cols = (2 * HD) // head_count
    out_cols = output_weight.shape[1]
    wq_piece = lax.dynamic_slice_in_dim(query_weight, head_index * q_cols, q_cols, axis=1)
    wkv_piece = lax.dynamic_slice_in_dim(keyvalue_weight, head_index * kv_cols, kv_cols, axis=1)
    proj_piece = jnp.concatenate([wq_piece, wkv_piece], axis=1)
    width = proj_piece.shape[1]
    wo_flat = output_weight.reshape(-1)
    wo_rows = -(-wo_flat.shape[0] // width)
    wo_rows = -(-(part_rows + wo_rows) // 8) * 8 - part_rows
    wo_block = jnp.pad(wo_flat, (0, wo_rows * width - wo_flat.shape[0])).reshape(wo_rows, width)
    piece = jnp.concatenate([proj_piece, wo_block], axis=0)
    stacked = grid_gather(piece)
    tok_count = stacked.shape[0]
    proj_w = stacked[:, :part_rows].reshape(tok_count * part_rows, width)
    wo_cols = (
        stacked[:, part_rows:]
        .reshape(tok_count, -1)[:, : wo_flat.shape[0]]
        .reshape(tok_count, HQ * HD, out_cols)
        .transpose(1, 0, 2)
        .reshape(HQ * HD, tok_count * out_cols)
    )
    gathered = lax.all_gather(tokens, "head", axis=1, tiled=True)
    wide = gathered.astype(jnp.float32)
    mean_square = jnp.mean(wide * wide, axis=1, keepdims=True)
    normed = (wide * lax.rsqrt(mean_square + 1e-06)).astype(jnp.bfloat16)
    both = jnp.dot(normed, proj_w, preferred_element_type=jnp.float32)
    mine = lax.all_to_all(both, "head", 0, 1, tiled=True)
    mine = mine.reshape(DRAFT, head_count, q_cols + kv_cols)
    q_pre = mine[:, :, :q_cols].reshape(DRAFT, HQ, HD)
    kv_pre = mine[:, :, q_cols:].reshape(DRAFT, 2 * HD)
    parent_row = lax.dynamic_index_in_dim(parents, head_index, 0, keepdims=False)
    length = lax.dynamic_index_in_dim(cache_len, head_index, 0, keepdims=False)
    leaf = lax.dynamic_index_in_dim(accepted_leaf, head_index, 0, keepdims=False)
    reach, depth = ancestry(parent_row)
    position = length + depth
    queries = (rotate(q_pre, position[:, None]) * HD ** (-0.5)).astype(jnp.bfloat16)
    tree_keys = rotate(kv_pre[:, :HD], position).astype(jnp.bfloat16)
    tree_values = kv_pre[:, HD:].astype(jnp.bfloat16)
    device = tok_index * head_count + head_index
    own_table = (
        lax.dynamic_index_in_dim(page_table, head_index, 0, keepdims=False) - device * pages_dev
    )
    own_pages = jnp.take(cache, own_table, axis=0)
    cache_keys = own_pages[:, 0].reshape(NPR * PAGE, HD)
    cache_values = own_pages[:, 1].reshape(NPR * PAGE, HD)
    result = attend(
        queries[None],
        cache_keys[None],
        cache_values[None],
        tree_keys[None],
        tree_values[None],
        length[None],
        position[None],
        reach[None],
    )
    mixed = lax.all_gather(result.reshape(DRAFT, HQ * HD), "head", axis=0, tiled=True)
    per_head = lax.dot_general(
        mixed.reshape(mixed.shape[0], HQ, HD),
        wo_cols.reshape(HQ, HD, wo_cols.shape[1]),
        (((2,), (1,)), ((1,), (0,))),
        preferred_element_type=jnp.float32,
    )
    summed = None
    for group in range(head_count):
        head_ids = [k for k in range(group, HQ, head_count)]
        if not head_ids:
            continue
        partial_value = per_head[head_ids[0]]
        for k in head_ids[1:]:
            partial_value = partial_value + per_head[k]
        term = partial_value.astype(jnp.bfloat16).astype(jnp.float32)
        summed = term if summed is None else summed + term
    attended = summed.astype(jnp.bfloat16)
    new_pages = refresh(own_pages, length, leaf, reach, depth, tree_keys, tree_values)
    matches = (own_table[:, None] == jnp.arange(pages_dev, dtype=jnp.int32)[None, :]).astype(
        jnp.int32
    )
    inverse = jnp.sum(matches * jnp.arange(pages_dev, dtype=jnp.int32)[:, None], axis=0)
    cache_out = jnp.take(new_pages, inverse, axis=0)
    return (attended, cache_out)


def solution(mesh):
    tok_size = mesh.shape["tok"]
    tx_size = 4 if tok_size % 4 == 0 else tok_size
    grid = Mesh(
        mesh.devices.reshape(tok_size // tx_size, tx_size, mesh.shape["head"]),
        ("tz", "tx", "head"),
    )
    tok = ("tz", "tx")
    in_specs = (
        P(tok, "head"),
        P(tok, None),
        P(tok, None),
        P(None, ("head",) + tok),
        P(tok + ("head",), None, None, None),
        P(tok, None),
        P(tok, None),
        P(tok),
        P(tok),
    )
    out_specs = (P(tok, "head"), P(tok + ("head",), None, None, None))
    return jax.shard_map(shards, mesh=grid, in_specs=in_specs, out_specs=out_specs, check_vma=False)
```

```python
import math

import jax
import jax.numpy as jnp
from jax import lax
from jax.sharding import Mesh, PartitionSpec as P

HQ = 10
HD = 256
DRAFT = 64
PAGE = 128
NPR = 4
WINDOW = 256


def ancestry(parent_row):
    node_ids = jnp.arange(DRAFT, dtype=jnp.int32)
    link = (parent_row[:, None] == node_ids[None, :]).astype(jnp.float32)
    reach = jnp.minimum(link + jnp.eye(DRAFT, dtype=jnp.float32), 1.0)
    for sweep in range((DRAFT - 1).bit_length()):
        reach = jnp.minimum(jnp.dot(reach, reach, precision=lax.Precision.HIGHEST), 1.0)
    depth = (jnp.sum(reach, axis=1) - 1.0).astype(jnp.int32)
    return (reach, depth)


def rotate(values, position):
    half = HD // 4
    freq = jnp.exp(jnp.arange(half, dtype=jnp.float32) * (-2.0 * math.log(10000.0) / (HD // 2)))
    angle = position.astype(jnp.float32)[..., None] * freq
    cosine = jnp.cos(angle)
    sine = jnp.sin(angle)
    first = values[..., :half]
    second = values[..., half : 2 * half]
    return jnp.concatenate(
        [first * cosine - second * sine, second * cosine + first * sine, values[..., 2 * half :]],
        axis=-1,
    )


def attend(queries, cache_keys, cache_values, tree_keys, tree_values, lengths, position, reach):
    window_span = cache_keys.shape[1]
    slot_ids = jnp.arange(window_span, dtype=jnp.int32)
    visible = (slot_ids[None, None, :] < lengths[:, None, None]) & (
        slot_ids[None, None, :] > position[:, :, None] - WINDOW
    )
    cache_scores = jnp.einsum(
        "rnhd,rcd->rhnc", queries, cache_keys, preferred_element_type=jnp.float32
    )
    tree_scores = jnp.einsum(
        "rnhd,rmd->rhnm", queries, tree_keys, preferred_element_type=jnp.float32
    )
    cache_scores = jnp.where(visible[:, None], cache_scores, -1e30)
    tree_scores = jnp.where(reach[:, None] > 0.5, tree_scores, -1e30)
    row_peak = jnp.maximum(jnp.max(cache_scores, axis=-1), jnp.max(tree_scores, axis=-1))[..., None]
    cache_weights = jnp.exp(cache_scores - row_peak)
    tree_weights = jnp.exp(tree_scores - row_peak)
    denominator = jnp.sum(cache_weights, axis=-1, keepdims=True) + jnp.sum(
        tree_weights, axis=-1, keepdims=True
    )
    cache_weights = (cache_weights / denominator).astype(jnp.bfloat16)
    tree_weights = (tree_weights / denominator).astype(jnp.bfloat16)
    result = jnp.einsum(
        "rhnc,rcd->rhnd", cache_weights, cache_values, preferred_element_type=jnp.float32
    )
    result = result + jnp.einsum(
        "rhnm,rmd->rhnd", tree_weights, tree_values, preferred_element_type=jnp.float32
    )
    return result.astype(jnp.bfloat16)


def refresh(logical_pages, length, leaf, reach, depth, new_keys, new_values):
    count = logical_pages.shape[0] * logical_pages.shape[2]
    logical = jnp.transpose(logical_pages, (1, 0, 2, 3)).reshape(2, count, HD)
    slot_ids = jnp.arange(count, dtype=jnp.int32)
    on_path = reach[leaf]
    selector = ((on_path[None, :] > 0.5) & (depth[None, :] == slot_ids[:, None] - length)).astype(
        jnp.float32
    )
    placed_keys = jnp.dot(selector, new_keys.astype(jnp.float32), precision=lax.Precision.HIGHEST)
    placed_values = jnp.dot(
        selector, new_values.astype(jnp.float32), precision=lax.Precision.HIGHEST
    )
    placed = jnp.stack([placed_keys, placed_values]).astype(jnp.bfloat16)
    written = jnp.sum(selector, axis=1) > 0.5
    logical = jnp.where(written[None, :, None], placed, logical)
    return jnp.transpose(
        logical.reshape(2, logical_pages.shape[0], logical_pages.shape[2], HD), (1, 0, 2, 3)
    )


def ring_pieces(piece, axis):
    size = lax.axis_size(axis)
    got = [(0, 0, piece)]
    ahead = piece
    behind = piece
    forward = [(i, (i + 1) % size) for i in range(size)]
    backward = [(i, (i - 1) % size) for i in range(size)]
    for step in range(1, size // 2 + 1):
        if 2 * step == size and size > 2:
            half = piece.shape[0] // 2
            got.append((step, 0, lax.ppermute(ahead[:half], axis, forward)))
            got.append((step, half, lax.ppermute(behind[half:], axis, backward)))
            break
        ahead = lax.ppermute(ahead, axis, forward)
        got.append((size - step, 0, ahead))
        if step <= (size - 1) // 2:
            behind = lax.ppermute(behind, axis, backward)
            got.append((step, 0, behind))
    return got


def grid_gather(piece):
    z_size = lax.axis_size("tz")
    x_size = lax.axis_size("tx")
    z_index = lax.axis_index("tz")
    x_index = lax.axis_index("tx")
    zero = jnp.int32(0)
    column = jnp.zeros((z_size,) + piece.shape, piece.dtype)
    for offset, first, part in ring_pieces(piece, "tz"):
        column = lax.dynamic_update_slice(
            column, part[None], ((z_index + offset) % z_size, jnp.int32(first), zero)
        )
    placed = jnp.zeros((z_size, x_size) + piece.shape, piece.dtype)
    for offset, first, part in ring_pieces(column, "tx"):
        placed = lax.dynamic_update_slice(
            placed, part[:, None], (jnp.int32(first), (x_index + offset) % x_size, zero, zero)
        )
    return placed.reshape((z_size * x_size,) + piece.shape)


def shards(
    tokens,
    query_weight,
    keyvalue_weight,
    output_weight,
    cache,
    page_table,
    parents,
    cache_len,
    accepted_leaf,
):
    head_count = lax.axis_size("head")
    head_index = lax.axis_index("head")
    tok_index = lax.axis_index("tz") * lax.axis_size("tx") + lax.axis_index("tx")
    requests = parents.shape[0]
    assert requests == head_count
    pages_dev = cache.shape[0]
    part_rows = query_weight.shape[0]
    q_cols = (HQ * HD) // head_count
    kv_cols = (2 * HD) // head_count
    out_cols = output_weight.shape[1]
    wq_piece = lax.dynamic_slice_in_dim(query_weight, head_index * q_cols, q_cols, axis=1)
    wkv_piece = lax.dynamic_slice_in_dim(keyvalue_weight, head_index * kv_cols, kv_cols, axis=1)
    proj_piece = jnp.concatenate([wq_piece, wkv_piece], axis=1)
    width = proj_piece.shape[1]
    wo_flat = output_weight.reshape(-1)
    wo_rows = -(-wo_flat.shape[0] // width)
    wo_rows = -(-(part_rows + wo_rows) // 8) * 8 - part_rows
    wo_block = jnp.pad(wo_flat, (0, wo_rows * width - wo_flat.shape[0])).reshape(wo_rows, width)
    piece = jnp.concatenate([proj_piece, wo_block], axis=0)
    stacked = grid_gather(piece)
    tok_count = stacked.shape[0]
    proj_w = stacked[:, :part_rows].reshape(tok_count * part_rows, width)
    wo_cols = (
        stacked[:, part_rows:]
        .reshape(tok_count, -1)[:, : wo_flat.shape[0]]
        .reshape(tok_count, HQ * HD, out_cols)
        .transpose(1, 0, 2)
        .reshape(HQ * HD, tok_count * out_cols)
    )
    gathered = lax.all_gather(tokens, "head", axis=1, tiled=True)
    wide = gathered.astype(jnp.float32)
    mean_square = jnp.mean(wide * wide, axis=1, keepdims=True)
    normed = (wide * lax.rsqrt(mean_square + 1e-06)).astype(jnp.bfloat16)
    both = jnp.dot(normed, proj_w, preferred_element_type=jnp.float32)
    mine = lax.all_to_all(both, "head", 0, 1, tiled=True)
    mine = mine.reshape(DRAFT, head_count, q_cols + kv_cols)
    q_pre = mine[:, :, :q_cols].reshape(DRAFT, HQ, HD)
    kv_pre = mine[:, :, q_cols:].reshape(DRAFT, 2 * HD)
    parent_row = lax.dynamic_index_in_dim(parents, head_index, 0, keepdims=False)
    length = lax.dynamic_index_in_dim(cache_len, head_index, 0, keepdims=False)
    leaf = lax.dynamic_index_in_dim(accepted_leaf, head_index, 0, keepdims=False)
    reach, depth = ancestry(parent_row)
    position = length + depth
    queries = (rotate(q_pre, position[:, None]) * HD ** (-0.5)).astype(jnp.bfloat16)
    tree_keys = rotate(kv_pre[:, :HD], position).astype(jnp.bfloat16)
    tree_values = kv_pre[:, HD:].astype(jnp.bfloat16)
    device = tok_index * head_count + head_index
    own_table = (
        lax.dynamic_index_in_dim(page_table, head_index, 0, keepdims=False) - device * pages_dev
    )
    own_pages = jnp.take(cache, own_table, axis=0)
    cache_keys = own_pages[:, 0].reshape(NPR * PAGE, HD)
    cache_values = own_pages[:, 1].reshape(NPR * PAGE, HD)
    result = attend(
        queries[None],
        cache_keys[None],
        cache_values[None],
        tree_keys[None],
        tree_values[None],
        length[None],
        position[None],
        reach[None],
    )
    mixed = lax.all_gather(result[0], "head", axis=1, tiled=True)
    per_head = lax.dot_general(
        mixed,
        wo_cols.reshape(HQ, HD, wo_cols.shape[1]),
        (((2,), (1,)), ((0,), (0,))),
        preferred_element_type=jnp.float32,
    )
    summed = None
    for group in range(head_count):
        head_ids = [k for k in range(group, HQ, head_count)]
        if not head_ids:
            continue
        partial_value = per_head[head_ids[0]]
        for k in head_ids[1:]:
            partial_value = partial_value + per_head[k]
        term = partial_value.astype(jnp.bfloat16).astype(jnp.float32)
        summed = term if summed is None else summed + term
    attended = summed.astype(jnp.bfloat16)
    new_pages = refresh(own_pages, length, leaf, reach, depth, tree_keys, tree_values)
    matches = (own_table[:, None] == jnp.arange(pages_dev, dtype=jnp.int32)[None, :]).astype(
        jnp.int32
    )
    inverse = jnp.sum(matches * jnp.arange(pages_dev, dtype=jnp.int32)[:, None], axis=0)
    cache_out = jnp.take(new_pages, inverse, axis=0)
    return (attended, cache_out)


def solution(mesh):
    tok_size = mesh.shape["tok"]
    tx_size = 4 if tok_size % 4 == 0 else tok_size
    grid = Mesh(
        mesh.devices.reshape(tok_size // tx_size, tx_size, mesh.shape["head"]),
        ("tz", "tx", "head"),
    )
    tok = ("tz", "tx")
    in_specs = (
        P(tok, "head"),
        P(tok, None),
        P(tok, None),
        P(None, ("head",) + tok),
        P(tok + ("head",), None, None, None),
        P(tok, None),
        P(tok, None),
        P(tok),
        P(tok),
    )
    out_specs = (P(tok, "head"), P(tok + ("head",), None, None, None))
    return jax.shard_map(shards, mesh=grid, in_specs=in_specs, out_specs=out_specs, check_vma=False)
```

```python
import math

import jax
import jax.numpy as jnp
from jax import lax
from jax.sharding import Mesh, PartitionSpec as P

HQ = 10
HD = 256
DRAFT = 64
PAGE = 128
NPR = 4
WINDOW = 256


def ancestry(parent_row):
    node_ids = jnp.arange(DRAFT, dtype=jnp.int32)
    link = (parent_row[:, None] == node_ids[None, :]).astype(jnp.float32)
    reach = jnp.minimum(link + jnp.eye(DRAFT, dtype=jnp.float32), 1.0)
    for sweep in range((DRAFT - 1).bit_length()):
        reach = jnp.minimum(jnp.dot(reach, reach, precision=lax.Precision.HIGHEST), 1.0)
    depth = (jnp.sum(reach, axis=1) - 1.0).astype(jnp.int32)
    return (reach, depth)


def rotate(values, position):
    half = HD // 4
    freq = jnp.exp(jnp.arange(half, dtype=jnp.float32) * (-2.0 * math.log(10000.0) / (HD // 2)))
    angle = position.astype(jnp.float32)[..., None] * freq
    cosine = jnp.cos(angle)
    sine = jnp.sin(angle)
    first = values[..., :half]
    second = values[..., half : 2 * half]
    return jnp.concatenate(
        [first * cosine - second * sine, second * cosine + first * sine, values[..., 2 * half :]],
        axis=-1,
    )


def attend(queries, cache_keys, cache_values, tree_keys, tree_values, lengths, position, reach):
    window_span = cache_keys.shape[1]
    slot_ids = jnp.arange(window_span, dtype=jnp.int32)
    visible = (slot_ids[None, None, :] < lengths[:, None, None]) & (
        slot_ids[None, None, :] > position[:, :, None] - WINDOW
    )
    cache_scores = jnp.einsum(
        "rnhd,rcd->rhnc", queries, cache_keys, preferred_element_type=jnp.float32
    )
    tree_scores = jnp.einsum(
        "rnhd,rmd->rhnm", queries, tree_keys, preferred_element_type=jnp.float32
    )
    cache_scores = jnp.where(visible[:, None], cache_scores, -1e30)
    tree_scores = jnp.where(reach[:, None] > 0.5, tree_scores, -1e30)
    row_peak = jnp.maximum(jnp.max(cache_scores, axis=-1), jnp.max(tree_scores, axis=-1))[..., None]
    cache_weights = jnp.exp(cache_scores - row_peak)
    tree_weights = jnp.exp(tree_scores - row_peak)
    denominator = jnp.sum(cache_weights, axis=-1, keepdims=True) + jnp.sum(
        tree_weights, axis=-1, keepdims=True
    )
    cache_weights = (cache_weights / denominator).astype(jnp.bfloat16)
    tree_weights = (tree_weights / denominator).astype(jnp.bfloat16)
    result = jnp.einsum(
        "rhnc,rcd->rhnd", cache_weights, cache_values, preferred_element_type=jnp.float32
    )
    result = result + jnp.einsum(
        "rhnm,rmd->rhnd", tree_weights, tree_values, preferred_element_type=jnp.float32
    )
    return result.astype(jnp.bfloat16)


def refresh(logical_pages, length, leaf, reach, depth, new_keys, new_values):
    count = logical_pages.shape[0] * logical_pages.shape[2]
    logical = jnp.transpose(logical_pages, (1, 0, 2, 3)).reshape(2, count, HD)
    slot_ids = jnp.arange(count, dtype=jnp.int32)
    on_path = reach[leaf]
    selector = ((on_path[None, :] > 0.5) & (depth[None, :] == slot_ids[:, None] - length)).astype(
        jnp.float32
    )
    placed_keys = jnp.dot(selector, new_keys.astype(jnp.float32), precision=lax.Precision.HIGHEST)
    placed_values = jnp.dot(
        selector, new_values.astype(jnp.float32), precision=lax.Precision.HIGHEST
    )
    placed = jnp.stack([placed_keys, placed_values]).astype(jnp.bfloat16)
    written = jnp.sum(selector, axis=1) > 0.5
    logical = jnp.where(written[None, :, None], placed, logical)
    return jnp.transpose(
        logical.reshape(2, logical_pages.shape[0], logical_pages.shape[2], HD), (1, 0, 2, 3)
    )


def ring_pieces(piece, axis):
    size = lax.axis_size(axis)
    got = [(0, 0, piece)]
    ahead = piece
    behind = piece
    forward = [(i, (i + 1) % size) for i in range(size)]
    backward = [(i, (i - 1) % size) for i in range(size)]
    for step in range(1, size // 2 + 1):
        if 2 * step == size and size > 2:
            half = piece.shape[0] // 2
            got.append((step, 0, lax.ppermute(ahead[:half], axis, forward)))
            got.append((step, half, lax.ppermute(behind[half:], axis, backward)))
            break
        ahead = lax.ppermute(ahead, axis, forward)
        got.append((size - step, 0, ahead))
        if step <= (size - 1) // 2:
            behind = lax.ppermute(behind, axis, backward)
            got.append((step, 0, behind))
    return got


def grid_gather(piece):
    z_size = lax.axis_size("tz")
    x_size = lax.axis_size("tx")
    z_index = lax.axis_index("tz")
    x_index = lax.axis_index("tx")
    zero = jnp.int32(0)
    column = jnp.zeros((z_size,) + piece.shape, piece.dtype)
    for offset, first, part in ring_pieces(piece, "tz"):
        column = lax.dynamic_update_slice(
            column, part[None], ((z_index + offset) % z_size, jnp.int32(first), zero)
        )
    placed = jnp.zeros((z_size, x_size) + piece.shape, piece.dtype)
    for offset, first, part in ring_pieces(column, "tx"):
        placed = lax.dynamic_update_slice(
            placed, part[:, None], (jnp.int32(first), (x_index + offset) % x_size, zero, zero)
        )
    return placed.reshape((z_size * x_size,) + piece.shape)


def shards(
    tokens,
    query_weight,
    keyvalue_weight,
    output_weight,
    cache,
    page_table,
    parents,
    cache_len,
    accepted_leaf,
):
    head_count = lax.axis_size("head")
    head_index = lax.axis_index("head")
    tok_index = lax.axis_index("tz") * lax.axis_size("tx") + lax.axis_index("tx")
    requests = parents.shape[0]
    assert requests == head_count
    pages_dev = cache.shape[0]
    part_rows = query_weight.shape[0]
    q_cols = (HQ * HD) // head_count
    kv_cols = (2 * HD) // head_count
    out_cols = output_weight.shape[1]
    wq_piece = lax.dynamic_slice_in_dim(query_weight, head_index * q_cols, q_cols, axis=1)
    wkv_piece = lax.dynamic_slice_in_dim(keyvalue_weight, head_index * kv_cols, kv_cols, axis=1)
    proj_piece = jnp.concatenate([wq_piece, wkv_piece], axis=1)
    width = proj_piece.shape[1]
    wo_flat = output_weight.reshape(-1)
    wo_rows = -(-wo_flat.shape[0] // width)
    wo_rows = -(-(part_rows + wo_rows) // 8) * 8 - part_rows
    wo_block = jnp.pad(wo_flat, (0, wo_rows * width - wo_flat.shape[0])).reshape(wo_rows, width)
    piece = jnp.concatenate([proj_piece, wo_block], axis=0)
    stacked = grid_gather(piece)
    tok_count = stacked.shape[0]
    proj_w = stacked[:, :part_rows].reshape(tok_count * part_rows, width)
    wo_cols = (
        stacked[:, part_rows:]
        .reshape(tok_count, -1)[:, : wo_flat.shape[0]]
        .reshape(tok_count, HQ * HD, out_cols)
        .transpose(1, 0, 2)
        .reshape(HQ * HD, tok_count * out_cols)
    )
    gathered = lax.all_gather(tokens, "head", axis=1, tiled=True)
    wide = gathered.astype(jnp.float32)
    mean_square = jnp.mean(wide * wide, axis=1, keepdims=True)
    normed = (wide * lax.rsqrt(mean_square + 1e-06)).astype(jnp.bfloat16)
    both = jnp.dot(normed, proj_w, preferred_element_type=jnp.float32)
    mine = lax.all_to_all(both.astype(jnp.bfloat16), "head", 0, 1, tiled=True)
    mine = mine.reshape(DRAFT, head_count, q_cols + kv_cols).astype(jnp.float32)
    q_pre = mine[:, :, :q_cols].reshape(DRAFT, HQ, HD)
    kv_pre = mine[:, :, q_cols:].reshape(DRAFT, 2 * HD)
    parent_row = lax.dynamic_index_in_dim(parents, head_index, 0, keepdims=False)
    length = lax.dynamic_index_in_dim(cache_len, head_index, 0, keepdims=False)
    leaf = lax.dynamic_index_in_dim(accepted_leaf, head_index, 0, keepdims=False)
    reach, depth = ancestry(parent_row)
    position = length + depth
    queries = (rotate(q_pre, position[:, None]) * HD ** (-0.5)).astype(jnp.bfloat16)
    tree_keys = rotate(kv_pre[:, :HD], position).astype(jnp.bfloat16)
    tree_values = kv_pre[:, HD:].astype(jnp.bfloat16)
    device = tok_index * head_count + head_index
    own_table = (
        lax.dynamic_index_in_dim(page_table, head_index, 0, keepdims=False) - device * pages_dev
    )
    own_pages = jnp.take(cache, own_table, axis=0)
    cache_keys = own_pages[:, 0].reshape(NPR * PAGE, HD)
    cache_values = own_pages[:, 1].reshape(NPR * PAGE, HD)
    result = attend(
        queries[None],
        cache_keys[None],
        cache_values[None],
        tree_keys[None],
        tree_values[None],
        length[None],
        position[None],
        reach[None],
    )
    mixed = lax.all_gather(result[0], "head", axis=1, tiled=True)
    per_head = lax.dot_general(
        mixed,
        wo_cols.reshape(HQ, HD, wo_cols.shape[1]),
        (((2,), (1,)), ((0,), (0,))),
        preferred_element_type=jnp.float32,
    )
    summed = None
    for group in range(head_count):
        head_ids = [k for k in range(group, HQ, head_count)]
        if not head_ids:
            continue
        partial_value = per_head[head_ids[0]]
        for k in head_ids[1:]:
            partial_value = partial_value + per_head[k]
        term = partial_value.astype(jnp.bfloat16).astype(jnp.float32)
        summed = term if summed is None else summed + term
    attended = summed.astype(jnp.bfloat16)
    new_pages = refresh(own_pages, length, leaf, reach, depth, tree_keys, tree_values)
    matches = (own_table[:, None] == jnp.arange(pages_dev, dtype=jnp.int32)[None, :]).astype(
        jnp.int32
    )
    inverse = jnp.sum(matches * jnp.arange(pages_dev, dtype=jnp.int32)[:, None], axis=0)
    cache_out = jnp.take(new_pages, inverse, axis=0)
    return (attended, cache_out)


def solution(mesh):
    tok_size = mesh.shape["tok"]
    tx_size = 4 if tok_size % 4 == 0 else tok_size
    grid = Mesh(
        mesh.devices.reshape(tok_size // tx_size, tx_size, mesh.shape["head"]),
        ("tz", "tx", "head"),
    )
    tok = ("tz", "tx")
    in_specs = (
        P(tok, "head"),
        P(tok, None),
        P(tok, None),
        P(None, ("head",) + tok),
        P(tok + ("head",), None, None, None),
        P(tok, None),
        P(tok, None),
        P(tok),
        P(tok),
    )
    out_specs = (P(tok, "head"), P(tok + ("head",), None, None, None))
    return jax.shard_map(shards, mesh=grid, in_specs=in_specs, out_specs=out_specs, check_vma=False)
```

```python
import math

import jax
import jax.numpy as jnp
from jax import lax
from jax.sharding import Mesh, PartitionSpec as P

HQ = 10
HD = 256
DRAFT = 64
PAGE = 128
NPR = 4
WINDOW = 256


def ancestry(parent_row):
    node_ids = jnp.arange(DRAFT, dtype=jnp.int32)
    link = (parent_row[:, None] == node_ids[None, :]).astype(jnp.float32)
    reach = jnp.minimum(link + jnp.eye(DRAFT, dtype=jnp.float32), 1.0)
    for sweep in range((DRAFT - 1).bit_length()):
        reach = jnp.minimum(jnp.dot(reach, reach, precision=lax.Precision.HIGHEST), 1.0)
    depth = (jnp.sum(reach, axis=1) - 1.0).astype(jnp.int32)
    return (reach, depth)


def rotate(values, position):
    half = HD // 4
    freq = jnp.exp(jnp.arange(half, dtype=jnp.float32) * (-2.0 * math.log(10000.0) / (HD // 2)))
    angle = position.astype(jnp.float32)[..., None] * freq
    cosine = jnp.cos(angle)
    sine = jnp.sin(angle)
    first = values[..., :half]
    second = values[..., half : 2 * half]
    return jnp.concatenate(
        [first * cosine - second * sine, second * cosine + first * sine, values[..., 2 * half :]],
        axis=-1,
    )


def attend(queries, cache_keys, cache_values, tree_keys, tree_values, lengths, position, reach):
    window_span = cache_keys.shape[1]
    slot_ids = jnp.arange(window_span, dtype=jnp.int32)
    visible = (slot_ids[None, None, :] < lengths[:, None, None]) & (
        slot_ids[None, None, :] > position[:, :, None] - WINDOW
    )
    cache_scores = jnp.einsum(
        "rnhd,rcd->rhnc", queries, cache_keys, preferred_element_type=jnp.float32
    )
    tree_scores = jnp.einsum(
        "rnhd,rmd->rhnm", queries, tree_keys, preferred_element_type=jnp.float32
    )
    cache_scores = jnp.where(visible[:, None], cache_scores, -1e30)
    tree_scores = jnp.where(reach[:, None] > 0.5, tree_scores, -1e30)
    row_peak = jnp.maximum(jnp.max(cache_scores, axis=-1), jnp.max(tree_scores, axis=-1))[..., None]
    cache_weights = jnp.exp(cache_scores - row_peak)
    tree_weights = jnp.exp(tree_scores - row_peak)
    denominator = jnp.sum(cache_weights, axis=-1, keepdims=True) + jnp.sum(
        tree_weights, axis=-1, keepdims=True
    )
    cache_weights = (cache_weights / denominator).astype(jnp.bfloat16)
    tree_weights = (tree_weights / denominator).astype(jnp.bfloat16)
    result = jnp.einsum(
        "rhnc,rcd->rhnd", cache_weights, cache_values, preferred_element_type=jnp.float32
    )
    result = result + jnp.einsum(
        "rhnm,rmd->rhnd", tree_weights, tree_values, preferred_element_type=jnp.float32
    )
    return result.astype(jnp.bfloat16)


def refresh(logical_pages, length, leaf, reach, depth, new_keys, new_values):
    count = logical_pages.shape[0] * logical_pages.shape[2]
    logical = jnp.transpose(logical_pages, (1, 0, 2, 3)).reshape(2, count, HD)
    slot_ids = jnp.arange(count, dtype=jnp.int32)
    on_path = reach[leaf]
    selector = ((on_path[None, :] > 0.5) & (depth[None, :] == slot_ids[:, None] - length)).astype(
        jnp.float32
    )
    placed_keys = jnp.dot(selector, new_keys.astype(jnp.float32), precision=lax.Precision.HIGHEST)
    placed_values = jnp.dot(
        selector, new_values.astype(jnp.float32), precision=lax.Precision.HIGHEST
    )
    placed = jnp.stack([placed_keys, placed_values]).astype(jnp.bfloat16)
    written = jnp.sum(selector, axis=1) > 0.5
    logical = jnp.where(written[None, :, None], placed, logical)
    return jnp.transpose(
        logical.reshape(2, logical_pages.shape[0], logical_pages.shape[2], HD), (1, 0, 2, 3)
    )


def ring_pieces(piece, axis):
    size = lax.axis_size(axis)
    got = [(0, 0, piece)]
    ahead = piece
    behind = piece
    forward = [(i, (i + 1) % size) for i in range(size)]
    backward = [(i, (i - 1) % size) for i in range(size)]
    for step in range(1, size // 2 + 1):
        if 2 * step == size and size > 2:
            half = piece.shape[0] // 2
            got.append((step, 0, lax.ppermute(ahead[:half], axis, forward)))
            got.append((step, half, lax.ppermute(behind[half:], axis, backward)))
            break
        ahead = lax.ppermute(ahead, axis, forward)
        got.append((size - step, 0, ahead))
        if step <= (size - 1) // 2:
            behind = lax.ppermute(behind, axis, backward)
            got.append((step, 0, behind))
    return got


def grid_gather(piece, early):
    z_size = lax.axis_size("tz")
    x_size = lax.axis_size("tx")
    z_index = lax.axis_index("tz")
    x_index = lax.axis_index("tx")
    zero = jnp.int32(0)
    column = jnp.zeros((z_size,) + piece.shape, piece.dtype)
    for offset, first, part in ring_pieces(piece, "tz"):
        column = lax.dynamic_update_slice(
            column, part[None], ((z_index + offset) % z_size, jnp.int32(first), zero)
        )
    column, early = lax.optimization_barrier((column, early))
    placed = jnp.zeros((z_size, x_size) + piece.shape, piece.dtype)
    for offset, first, part in ring_pieces(column, "tx"):
        placed = lax.dynamic_update_slice(
            placed, part[:, None], (jnp.int32(first), (x_index + offset) % x_size, zero, zero)
        )
    return placed.reshape((z_size * x_size,) + piece.shape), early


def shards(
    tokens,
    query_weight,
    keyvalue_weight,
    output_weight,
    cache,
    page_table,
    parents,
    cache_len,
    accepted_leaf,
):
    head_count = lax.axis_size("head")
    head_index = lax.axis_index("head")
    tok_index = lax.axis_index("tz") * lax.axis_size("tx") + lax.axis_index("tx")
    requests = parents.shape[0]
    assert requests == head_count
    pages_dev = cache.shape[0]
    part_rows = query_weight.shape[0]
    q_cols = (HQ * HD) // head_count
    kv_cols = (2 * HD) // head_count
    out_cols = output_weight.shape[1]
    wq_piece = lax.dynamic_slice_in_dim(query_weight, head_index * q_cols, q_cols, axis=1)
    wkv_piece = lax.dynamic_slice_in_dim(keyvalue_weight, head_index * kv_cols, kv_cols, axis=1)
    proj_piece = jnp.concatenate([wq_piece, wkv_piece], axis=1)
    width = proj_piece.shape[1]
    wo_flat = output_weight.reshape(-1)
    wo_rows = -(-wo_flat.shape[0] // width)
    wo_rows = -(-(part_rows + wo_rows) // 8) * 8 - part_rows
    wo_block = jnp.pad(wo_flat, (0, wo_rows * width - wo_flat.shape[0])).reshape(wo_rows, width)
    piece = jnp.concatenate([proj_piece, wo_block], axis=0)
    gathered = lax.all_gather(tokens, "head", axis=1, tiled=True)
    wide = gathered.astype(jnp.float32)
    mean_square = jnp.mean(wide * wide, axis=1, keepdims=True)
    normed = (wide * lax.rsqrt(mean_square + 1e-06)).astype(jnp.bfloat16)
    stacked, normed = grid_gather(piece, normed)
    tok_count = stacked.shape[0]
    proj_w = stacked[:, :part_rows].reshape(tok_count * part_rows, width)
    wo_cols = (
        stacked[:, part_rows:]
        .reshape(tok_count, -1)[:, : wo_flat.shape[0]]
        .reshape(tok_count, HQ * HD, out_cols)
        .transpose(1, 0, 2)
        .reshape(HQ * HD, tok_count * out_cols)
    )
    both = jnp.dot(normed, proj_w, preferred_element_type=jnp.float32)
    mine = lax.all_to_all(both, "head", 0, 1, tiled=True)
    mine = mine.reshape(DRAFT, head_count, q_cols + kv_cols)
    q_pre = mine[:, :, :q_cols].reshape(DRAFT, HQ, HD)
    kv_pre = mine[:, :, q_cols:].reshape(DRAFT, 2 * HD)
    parent_row = lax.dynamic_index_in_dim(parents, head_index, 0, keepdims=False)
    length = lax.dynamic_index_in_dim(cache_len, head_index, 0, keepdims=False)
    leaf = lax.dynamic_index_in_dim(accepted_leaf, head_index, 0, keepdims=False)
    reach, depth = ancestry(parent_row)
    position = length + depth
    queries = (rotate(q_pre, position[:, None]) * HD ** (-0.5)).astype(jnp.bfloat16)
    tree_keys = rotate(kv_pre[:, :HD], position).astype(jnp.bfloat16)
    tree_values = kv_pre[:, HD:].astype(jnp.bfloat16)
    device = tok_index * head_count + head_index
    own_table = (
        lax.dynamic_index_in_dim(page_table, head_index, 0, keepdims=False) - device * pages_dev
    )
    own_pages = jnp.take(cache, own_table, axis=0)
    cache_keys = own_pages[:, 0].reshape(NPR * PAGE, HD)
    cache_values = own_pages[:, 1].reshape(NPR * PAGE, HD)
    result = attend(
        queries[None],
        cache_keys[None],
        cache_values[None],
        tree_keys[None],
        tree_values[None],
        length[None],
        position[None],
        reach[None],
    )
    mixed = lax.all_gather(result[0], "head", axis=1, tiled=True)
    per_head = lax.dot_general(
        mixed,
        wo_cols.reshape(HQ, HD, wo_cols.shape[1]),
        (((2,), (1,)), ((0,), (0,))),
        preferred_element_type=jnp.float32,
    )
    summed = None
    for group in range(head_count):
        head_ids = [k for k in range(group, HQ, head_count)]
        if not head_ids:
            continue
        partial_value = per_head[head_ids[0]]
        for k in head_ids[1:]:
            partial_value = partial_value + per_head[k]
        term = partial_value.astype(jnp.bfloat16).astype(jnp.float32)
        summed = term if summed is None else summed + term
    attended = summed.astype(jnp.bfloat16)
    new_pages = refresh(own_pages, length, leaf, reach, depth, tree_keys, tree_values)
    matches = (own_table[:, None] == jnp.arange(pages_dev, dtype=jnp.int32)[None, :]).astype(
        jnp.int32
    )
    inverse = jnp.sum(matches * jnp.arange(pages_dev, dtype=jnp.int32)[:, None], axis=0)
    cache_out = jnp.take(new_pages, inverse, axis=0)
    return (attended, cache_out)


def solution(mesh):
    tok_size = mesh.shape["tok"]
    tx_size = 4 if tok_size % 4 == 0 else tok_size
    grid = Mesh(
        mesh.devices.reshape(tok_size // tx_size, tx_size, mesh.shape["head"]),
        ("tz", "tx", "head"),
    )
    tok = ("tz", "tx")
    in_specs = (
        P(tok, "head"),
        P(tok, None),
        P(tok, None),
        P(None, ("head",) + tok),
        P(tok + ("head",), None, None, None),
        P(tok, None),
        P(tok, None),
        P(tok),
        P(tok),
    )
    out_specs = (P(tok, "head"), P(tok + ("head",), None, None, None))
    return jax.shard_map(shards, mesh=grid, in_specs=in_specs, out_specs=out_specs, check_vma=False)
```
